128 devices in a mesh: tm: 4 (over y_hi, core), space: 32 (over x, y_lo, z).
Axes of the slice: x: 4, y: 4 (y_hi: 2, y_lo: 2; y = y_hi * 2 + y_lo), z: 4, core: 2. Of those that a mesh axis runs over, the one named last changes fastest.
Arguments:
- query_rows: bfloat16 [32768, 2560], P(('tm', 'space')), may hold values from -18 to 18
- key_rows: bfloat16 [32768, 2560], P(('tm', 'space')), may hold values from -7 to 7
- value_rows: bfloat16 [32768, 2560], P(('tm', 'space')), may hold values from -12 to 12
- out_cotangent: bfloat16 [32768, 2560], P(('tm', 'space')), may hold values from -12 to 12
- tile_slot: int32 [32768], P(('tm', 'space')), may hold values from 0 to 32767, as said below
- window_reach: int32 [4, 32, 2], P(None, 'space'), may hold values from 0 to 1, as said below
Outputs:
- attended: bfloat16 [32768, 2560], P(('tm', 'space'))
- query_grad: bfloat16 [32768, 2560], P(('tm', 'space'))
- key_grad: bfloat16 [32768, 2560], P(('tm', 'space'))
- value_grad: bfloat16 [32768, 2560], P(('tm', 'space'))
The draws below stay inside these ranges and needn't reach their ends.
Inputs may be any that keep to these rules, and one draw needn't show every extreme that they name: `tile_slot`: A permutation of the tile-order positions. The raster tokens r * 256 to r * 256 + 256 - 1 (shard r, counted over tm first, then space) take, for every shard d, exactly the 2 positions d * 256 + r * 2 to d * 256 + r * 2 + 1. `window_reach`: entry 0 is 0 in the lowest slab and entry 1 is 0 in the highest slab.
All inputs are finite; a program needn't handle non-finite values.
Results may differ from the reference program's by a relative error of at most 0.0053.
Values may be sent and summed in bfloat16 or wider, within the bound.
No kernel may reach another device: no remote copies, remote signals or barrier semaphores. Data moves between devices by JAX's collectives and lax.ppermute only.
A program may use at most 192 MiB of HBM per device.

```python
import jax
import jax.numpy as jnp
from jax import lax

H = 20
HD = 128
TILE = 256
TILES_DEV = 1
TOK_DEV = 256
TOKENS = 32768
N_TM = 4
N_SPACE = 32


def balanced_slots(seed_key):
    shard_count = N_TM * N_SPACE
    per_peer = TOK_DEV // shard_count
    shard_keys = jax.random.split(seed_key, shard_count)

    def one_shard(shard_key, shard_index):
        shuffled = jax.random.permutation(shard_key, TOK_DEV)
        inverse = jnp.argsort(shuffled).astype(jnp.int32)
        return inverse // per_peer * TOK_DEV + shard_index * per_peer + inverse % per_peer
    slots = jax.vmap(one_shard)(shard_keys, jnp.arange(shard_count, dtype=jnp.int32))
    return slots.reshape(-1).astype(jnp.int32)


def draw_tile_slot(key, part):
    return balanced_slots(jax.random.fold_in(key, 11))


def draw_window_reach(key, part):
    columns = N_SPACE * TILES_DEV
    coin_flips = (jax.random.randint(jax.random.fold_in(key, 23), (N_TM, columns, 2), 0, 4) > 0).astype(jnp.int32)
    slab_index = jnp.arange(N_TM)[:, None, None]
    which_side = jnp.arange(2)[None, None, :]
    border = (slab_index == 0) & (which_side == 0) | (slab_index == N_TM - 1) & (which_side == 1)
    return jnp.where(border, 0, coin_flips).astype(jnp.int32)


def draw_query_rows(key, part):
    drawn = 1.5 * jnp.clip(jax.random.normal(jax.random.fold_in(key, 31), (TOKENS, H * HD), jnp.float32), -6.0, 6.0)
    return drawn.astype(jnp.bfloat16)


def draw_key_rows(key, part):
    drawn = jnp.clip(jax.random.normal(jax.random.fold_in(key, 41), (TOKENS, H * HD), jnp.float32), -6.0, 6.0)
    return drawn.astype(jnp.bfloat16)


def block_levels(key, shape, cuts, smallest, top_value):
    loudness = 1.0
    for dim, blocks in cuts:
        heights = jax.random.uniform(jax.random.fold_in(jax.random.fold_in(key, 6), dim), (blocks,), jnp.float32, smallest / len(cuts), top_value / len(cuts))
        loudness = loudness * jnp.repeat(jnp.exp(heights), shape[dim] // blocks).reshape((-1,) + (1,) * (len(shape) - 1 - dim))
    return loudness


def bell_draw(stream_key, shape, scale, limit, pieces=(), kind=jnp.bfloat16):
    entries = scale * jax.random.normal(stream_key, shape, jnp.float32)
    if pieces:
        entries = entries * block_levels(stream_key, shape, pieces, -0.22, 0.18)
    return jnp.clip(entries, -limit, limit).astype(kind)


def setup_inputs(seed: int = 0) -> dict:
    seeds = jax.random.split(jax.random.key(seed), 7)
    return {
        "query_rows": draw_query_rows(jax.random.fold_in(seeds[6], 71), 0),
        "key_rows": draw_key_rows(jax.random.fold_in(seeds[6], 71), 0),
        "value_rows": bell_draw(seeds[2], (TOKENS, H * HD), 2.0, 12.0, ((0, 128),)),
        "out_cotangent": bell_draw(seeds[3], (TOKENS, H * HD), 2.0, 12.0, ((0, 128),)),
        "tile_slot": draw_tile_slot(jax.random.fold_in(seeds[6], 71), 0),
        "window_reach": draw_window_reach(jax.random.fold_in(seeds[6], 71), 0),
    }


def rounded(values):
    return lax.optimization_barrier(values.astype(jnp.bfloat16)).astype(jnp.float32)


def pick_five(piece):
    return jnp.stack([piece[0, 1], piece[1, 1], piece[2, 1], piece[1, 0], piece[1, 2]])


def start_of(*values):
    return tuple(jnp.asarray(value).astype(jnp.int32) for value in values)


def reference(query_rows, key_rows, value_rows, out_cotangent, tile_slot, window_reach):
    softmax_scale = HD ** -0.5
    columns = N_SPACE * TILES_DEV
    tile_count = N_TM * columns
    source_of = jnp.zeros((TOKENS,), jnp.int32).at[tile_slot].set(jnp.arange(TOKENS, dtype=jnp.int32))

    def tiled(array):
        shaped = array[source_of].reshape(N_TM, columns, TILE, H, HD)
        return jnp.pad(shaped, ((1, 1), (1, 1), (0, 0), (0, 0), (0, 0)))

    query_pad = tiled(query_rows)
    key_pad = tiled(key_rows)
    value_pad = tiled(value_rows)
    grad_pad = tiled(out_cotangent)
    border = jnp.zeros((1, columns, 2), jnp.int32)
    reach_pad = jnp.concatenate([border, window_reach.astype(jnp.int32), border], axis=0)

    def take_five(array, slab_index, column):
        piece = lax.dynamic_slice(array, start_of(slab_index, column, 0, 0, 0), (3, 3, TILE, H, HD))
        return pick_five(piece).astype(jnp.float32)

    def take_own(array, slab_index, column):
        piece = lax.dynamic_slice(array, start_of(slab_index + 1, column + 1, 0, 0, 0), (1, 1, TILE, H, HD))
        return piece[0, 0].astype(jnp.float32)

    def forward_tile(tile_index):
        slab_index = (tile_index // columns).astype(jnp.int32)
        column = (tile_index % columns).astype(jnp.int32)
        keys_near = take_five(key_pad, slab_index, column)
        values_near = take_five(value_pad, slab_index, column)
        queries = take_own(query_pad, slab_index, column)
        cotangent = take_own(grad_pad, slab_index, column)
        reach_here = lax.dynamic_slice(reach_pad, start_of(slab_index + 1, column, 0), (1, 1, 2))[0, 0]
        allowed = jnp.stack([reach_here[0] > 0, reach_here[0] >= 0, reach_here[1] > 0, column > 0, column < columns - 1])
        visible = allowed[None, None, :, None]
        scores = jnp.einsum('qhd,akhd->hqak', queries, keys_near) * softmax_scale
        row_max = jnp.max(jnp.where(visible, scores, -1e30), axis=(2, 3), keepdims=True)
        expo = jnp.where(visible, jnp.exp(scores - row_max), 0.0)
        row_sum = jnp.sum(expo, axis=(2, 3), keepdims=True)
        weights = expo / row_sum
        weights_low = rounded(weights)
        output = jnp.einsum('hqak,akhd->qhd', weights_low, values_near).astype(jnp.bfloat16)
        dweights = jnp.einsum('qhd,akhd->hqak', cotangent, values_near)
        row_dot = jnp.sum(weights * dweights, axis=(2, 3), keepdims=True)
        dscores = rounded(weights * (dweights - row_dot) * softmax_scale)
        query_part = jnp.einsum('hqak,akhd->qhd', dscores, keys_near).astype(jnp.bfloat16)
        return output, query_part, row_max[:, :, 0, 0], row_sum[:, :, 0, 0], row_dot[:, :, 0, 0]

    outputs, query_parts, maxima, sums, dots = lax.map(forward_tile, jnp.arange(tile_count, dtype=jnp.int32))

    def stat_pad(stat, fill):
        shaped = stat.reshape(N_TM, columns, H, TILE)
        return jnp.pad(shaped, ((1, 1), (1, 1), (0, 0), (0, 0)), constant_values=fill)

    max_pad = stat_pad(maxima, 0.0)
    sum_pad = stat_pad(sums, 1.0)
    dot_pad = stat_pad(dots, 0.0)

    def backward_tile(tile_index):
        slab_index = (tile_index // columns).astype(jnp.int32)
        column = (tile_index % columns).astype(jnp.int32)
        queries = take_five(query_pad, slab_index, column)
        cotangent = take_five(grad_pad, slab_index, column)
        keys_here = take_own(key_pad, slab_index, column)
        values_here = take_own(value_pad, slab_index, column)
        reach_near = lax.dynamic_slice(reach_pad, start_of(slab_index, column, 0), (3, 1, 2))[:, 0]
        included = jnp.stack([reach_near[0, 1] > 0, reach_near[1, 0] >= 0, reach_near[2, 0] > 0, column > 0, column < columns - 1])
        visible = included[:, None, None, None]

        def stat_five(array):
            piece = lax.dynamic_slice(array, start_of(slab_index, column, 0, 0), (3, 3, H, TILE))
            return pick_five(piece)[..., None]

        row_max = stat_five(max_pad)
        row_sum = jnp.where(visible, stat_five(sum_pad), 1.0)
        row_dot = stat_five(dot_pad)
        scores = jnp.einsum('bqhd,khd->bhqk', queries, keys_here) * softmax_scale
        weights = jnp.where(visible, jnp.exp(scores - row_max) / row_sum, 0.0)
        weights_low = rounded(weights)
        dweights = jnp.einsum('bqhd,khd->bhqk', cotangent, values_here)
        dscores = rounded(weights * (dweights - row_dot) * softmax_scale)
        key_part = jnp.einsum('bhqk,bqhd->khd', dscores, queries).astype(jnp.bfloat16)
        value_part = jnp.einsum('bhqk,bqhd->khd', weights_low, cotangent).astype(jnp.bfloat16)
        return key_part, value_part

    key_parts, value_parts = lax.map(backward_tile, jnp.arange(tile_count, dtype=jnp.int32))

    def to_raster(array):
        return array.reshape(TOKENS, H * HD)[tile_slot]

    return (to_raster(outputs), to_raster(query_parts), to_raster(key_parts), to_raster(value_parts))
```

```python
import functools

import jax
import jax.numpy as jnp
from jax import lax
from jax.experimental import pallas as pl
from jax.experimental.pallas import tpu as pltpu
from jax.sharding import PartitionSpec as P

H = 20
HD = 128
TILE = 256
SETS = 5
NT_DIMS = (((1,), (1,)), ((), ()))


def _attn_kernel(flags_ref, q_ref, g_ref, k_ref, v_ref, kb_ref, ka_ref, kl_ref, kr_ref,
                 o_ref, dq_ref, dko_ref, dvo_ref, nb_b, nb_a, nb_l, nb_r, s_scr, dp_scr):
    scale = HD ** (-0.5)
    q = q_ref[...]
    g = g_ref[...]
    keys = [kb_ref[0], k_ref[...], ka_ref[0], kl_ref[0], kr_ref[0]]
    vals = [kb_ref[1], v_ref[...], ka_ref[1], kl_ref[1], kr_ref[1]]
    nb_out = [nb_b, None, nb_a, nb_l, nb_r]
    vis = [flags_ref[a] > 0 for a in range(SETS)]

    m = jnp.full((TILE, 1), -1e30, jnp.float32)
    for a in range(SETS):
        s = lax.dot_general(q, keys[a], NT_DIMS, preferred_element_type=jnp.float32) * scale
        s = jnp.where(vis[a], s, -1e30)
        s_scr[a] = s
        m = jnp.maximum(m, jnp.max(s, axis=1, keepdims=True))
    l = jnp.zeros((TILE, 1), jnp.float32)
    for a in range(SETS):
        e = jnp.where(vis[a], jnp.exp(s_scr[a] - m), 0.0)
        s_scr[a] = e
        l = l + jnp.sum(e, axis=1, keepdims=True)
    inv = 1.0 / l
    o = jnp.zeros((TILE, HD), jnp.float32)
    rd = jnp.zeros((TILE, 1), jnp.float32)
    for a in range(SETS):
        p = s_scr[a] * inv
        pb = p.astype(jnp.bfloat16)
        o = o + jnp.dot(pb, vals[a], preferred_element_type=jnp.float32)
        dp = lax.dot_general(g, vals[a], NT_DIMS, preferred_element_type=jnp.float32)
        rd = rd + jnp.sum(p * dp, axis=1, keepdims=True)
        s_scr[a] = p
        dp_scr[a] = dp
        dv = jnp.dot(p.T.astype(jnp.bfloat16), g, preferred_element_type=jnp.float32)
        if a == 1:
            dvo_ref[...] = dv
        else:
            nb_out[a][1] = dv.astype(jnp.bfloat16)
    o_ref[...] = o.astype(jnp.bfloat16)
    dq = jnp.zeros((TILE, HD), jnp.float32)
    for a in range(SETS):
        ds = s_scr[a] * (dp_scr[a] - rd) * scale
        dq = dq + jnp.dot(ds.astype(jnp.bfloat16), keys[a], preferred_element_type=jnp.float32)
        dk = jnp.dot(ds.T.astype(jnp.bfloat16), q, preferred_element_type=jnp.float32)
        if a == 1:
            dko_ref[...] = dk
        else:
            nb_out[a][0] = dk.astype(jnp.bfloat16)
    dq_ref[...] = dq.astype(jnp.bfloat16)


def attend_tile(flags, recv, kv_below, kv_above, kv_left, kv_right):
    tokens = recv.shape[0]
    own = lambda part: pl.BlockSpec((tokens, HD), lambda h, f, part=part: (0, part * H + h))
    pair = pl.BlockSpec((2, tokens, HD), lambda h, f: (0, 0, h))
    head = pl.BlockSpec((tokens, HD), lambda h, f: (0, h))
    flops = 6 * SETS * 2 * tokens * TILE * HD * H
    bytes_accessed = (4 * 2 + 4 * 4 + 4 * 2 * 2 + 2 * 2 + 2 * 4 + 4 * 2 * 2) * tokens * HD * H
    out_shape = (
        jax.ShapeDtypeStruct((tokens, H * HD), jnp.bfloat16),
        jax.ShapeDtypeStruct((tokens, H * HD), jnp.bfloat16),
        jax.ShapeDtypeStruct((tokens, H * HD), jnp.float32),
        jax.ShapeDtypeStruct((tokens, H * HD), jnp.float32),
    ) + tuple(jax.ShapeDtypeStruct((2, tokens, H * HD), jnp.bfloat16) for _ in range(4))
    return pl.pallas_call(
        _attn_kernel,
        out_shape=out_shape,
        grid_spec=pltpu.PrefetchScalarGridSpec(
            num_scalar_prefetch=1,
            grid=(H,),
            in_specs=[own(0), own(3), own(1), own(2), pair, pair, pair, pair],
            out_specs=[head, head, head, head, pair, pair, pair, pair],
            scratch_shapes=[
                pltpu.VMEM((SETS, tokens, TILE), jnp.float32),
                pltpu.VMEM((SETS, tokens, TILE), jnp.float32),
            ],
        ),
        compiler_params=pltpu.CompilerParams(dimension_semantics=("arbitrary",)),
        cost_estimate=pl.CostEstimate(
            flops=flops, transcendentals=SETS * tokens * TILE * H, bytes_accessed=bytes_accessed
        ),
    )(flags, recv, recv, recv, recv, kv_below, kv_above, kv_left, kv_right)


def shifted(block, axis, distance):
    devices = range(lax.axis_size(axis))
    route = [(i - distance, i) for i in devices if i - distance in devices]
    return lax.ppermute(block, axis, route)


def shards(query_rows, key_rows, value_rows, out_cotangent, tile_slot, window_reach):
    tokens_here, channels = query_rows.shape
    tm_count = lax.axis_size("tm")
    space_count = lax.axis_size("space")
    per_peer = tokens_here // (tm_count * space_count)
    own_rank = lax.axis_index("tm") * space_count + lax.axis_index("space")
    landing = tile_slot // tokens_here * per_peer + tile_slot % tokens_here - own_rank * per_peer
    chosen = (
        jnp.zeros((tokens_here,), jnp.int32)
        .at[landing]
        .set(jnp.arange(tokens_here, dtype=jnp.int32))
    )
    send = jnp.concatenate(
        [query_rows[chosen], key_rows[chosen], value_rows[chosen], out_cotangent[chosen]], axis=1
    )
    recv = lax.all_to_all(send, ("tm", "space"), split_axis=0, concat_axis=0, tiled=True)
    slab_index = lax.axis_index("tm")
    column = lax.axis_index("space")
    own_reach = lax.dynamic_index_in_dim(window_reach, slab_index, 0, keepdims=False)[0]
    flags = jnp.stack(
        [own_reach[0] > 0, own_reach[0] >= 0, own_reach[1] > 0, column > 0, column < space_count - 1]
    ).astype(jnp.int32)
    kv_own = jnp.stack([recv[:, channels:2 * channels], recv[:, 2 * channels:3 * channels]])
    kv_below = shifted(kv_own, "tm", 1)
    kv_above = shifted(kv_own, "tm", -1)
    kv_left = shifted(kv_own, "space", 1)
    kv_right = shifted(kv_own, "space", -1)
    attended, query_grad, key_own, value_own, nb_b, nb_a, nb_l, nb_r = attend_tile(
        flags, recv, kv_below, kv_above, kv_left, kv_right
    )
    from_above = shifted(nb_b, "tm", -1)
    from_below = shifted(nb_a, "tm", 1)
    from_right = shifted(nb_l, "space", -1)
    from_left = shifted(nb_r, "space", 1)
    terms = (
        from_above.astype(jnp.float32)
        + from_below.astype(jnp.float32)
        + from_right.astype(jnp.float32)
        + from_left.astype(jnp.float32)
    )
    key_grad = (key_own + terms[0]).astype(jnp.bfloat16)
    value_grad = (value_own + terms[1]).astype(jnp.bfloat16)
    out_tile = jnp.concatenate([attended, query_grad, key_grad, value_grad], axis=1)
    back = lax.all_to_all(out_tile, ("tm", "space"), split_axis=0, concat_axis=0, tiled=True)
    rows = back[landing]
    return tuple(rows[:, i * channels:(i + 1) * channels] for i in range(4))


def solution(mesh):
    return jax.shard_map(
        shards,
        mesh=mesh,
        in_specs=(
            P(("tm", "space"), None),
            P(("tm", "space"), None),
            P(("tm", "space"), None),
            P(("tm", "space"), None),
            P(("tm", "space")),
            P(None, "space", None),
        ),
        out_specs=(
            P(("tm", "space"), None),
            P(("tm", "space"), None),
            P(("tm", "space"), None),
            P(("tm", "space"), None),
        ),
        check_vma=False,
    )
```

```python
import functools

import jax
import jax.numpy as jnp
from jax import lax
from jax.experimental import pallas as pl
from jax.experimental.pallas import tpu as pltpu
from jax.sharding import PartitionSpec as P

H = 20
HD = 128
TILE = 256
SETS = 5
CHUNKS = 2
NT_DIMS = (((1,), (1,)), ((), ()))


def _attn_kernel(flags_ref, q_ref, g_ref, k_ref, v_ref, kb_ref, ka_ref, kl_ref, kr_ref,
                 o_ref, dq_ref, dko_ref, dvo_ref, nb_b, nb_a, nb_l, nb_r, s_scr, dp_scr):
    scale = HD ** (-0.5)
    q = q_ref[...]
    g = g_ref[...]
    keys = [kb_ref[0], k_ref[...], ka_ref[0], kl_ref[0], kr_ref[0]]
    vals = [kb_ref[1], v_ref[...], ka_ref[1], kl_ref[1], kr_ref[1]]
    nb_out = [nb_b, None, nb_a, nb_l, nb_r]
    vis = [flags_ref[a] > 0 for a in range(SETS)]

    m = jnp.full((TILE, 1), -1e30, jnp.float32)
    for a in range(SETS):
        s = lax.dot_general(q, keys[a], NT_DIMS, preferred_element_type=jnp.float32) * scale
        s = jnp.where(vis[a], s, -1e30)
        s_scr[a] = s
        m = jnp.maximum(m, jnp.max(s, axis=1, keepdims=True))
    l = jnp.zeros((TILE, 1), jnp.float32)
    for a in range(SETS):
        e = jnp.where(vis[a], jnp.exp(s_scr[a] - m), 0.0)
        s_scr[a] = e
        l = l + jnp.sum(e, axis=1, keepdims=True)
    inv = 1.0 / l
    o = jnp.zeros((TILE, HD), jnp.float32)
    rd = jnp.zeros((TILE, 1), jnp.float32)
    for a in range(SETS):
        p = s_scr[a] * inv
        pb = p.astype(jnp.bfloat16)
        o = o + jnp.dot(pb, vals[a], preferred_element_type=jnp.float32)
        dp = lax.dot_general(g, vals[a], NT_DIMS, preferred_element_type=jnp.float32)
        rd = rd + jnp.sum(p * dp, axis=1, keepdims=True)
        s_scr[a] = p
        dp_scr[a] = dp
        dv = jnp.dot(p.T.astype(jnp.bfloat16), g, preferred_element_type=jnp.float32)
        if a == 1:
            dvo_ref[...] = dv
        else:
            nb_out[a][1] = dv.astype(jnp.bfloat16)
    o_ref[...] = o.astype(jnp.bfloat16)
    dq = jnp.zeros((TILE, HD), jnp.float32)
    for a in range(SETS):
        ds = s_scr[a] * (dp_scr[a] - rd) * scale
        dq = dq + jnp.dot(ds.astype(jnp.bfloat16), keys[a], preferred_element_type=jnp.float32)
        dk = jnp.dot(ds.T.astype(jnp.bfloat16), q, preferred_element_type=jnp.float32)
        if a == 1:
            dko_ref[...] = dk
        else:
            nb_out[a][0] = dk.astype(jnp.bfloat16)
    dq_ref[...] = dq.astype(jnp.bfloat16)


def attend_tile(flags, recv, kv_below, kv_above, kv_left, kv_right):
    tokens = recv.shape[0]
    heads = recv.shape[1] // (4 * HD)
    own = lambda part: pl.BlockSpec((tokens, HD), lambda h, f, part=part: (0, part * heads + h))
    pair = pl.BlockSpec((2, tokens, HD), lambda h, f: (0, 0, h))
    head = pl.BlockSpec((tokens, HD), lambda h, f: (0, h))
    flops = 6 * SETS * 2 * tokens * TILE * HD * heads
    bytes_accessed = (4 * 2 + 4 * 4 + 4 * 2 * 2 + 2 * 2 + 2 * 4 + 4 * 2 * 2) * tokens * HD * heads
    out_shape = (
        jax.ShapeDtypeStruct((tokens, heads * HD), jnp.bfloat16),
        jax.ShapeDtypeStruct((tokens, heads * HD), jnp.bfloat16),
        jax.ShapeDtypeStruct((tokens, heads * HD), jnp.float32),
        jax.ShapeDtypeStruct((tokens, heads * HD), jnp.float32),
    ) + tuple(jax.ShapeDtypeStruct((2, tokens, heads * HD), jnp.bfloat16) for _ in range(4))
    return pl.pallas_call(
        _attn_kernel,
        out_shape=out_shape,
        grid_spec=pltpu.PrefetchScalarGridSpec(
            num_scalar_prefetch=1,
            grid=(heads,),
            in_specs=[own(0), own(3), own(1), own(2), pair, pair, pair, pair],
            out_specs=[head, head, head, head, pair, pair, pair, pair],
            scratch_shapes=[
                pltpu.VMEM((SETS, tokens, TILE), jnp.float32),
                pltpu.VMEM((SETS, tokens, TILE), jnp.float32),
            ],
        ),
        compiler_params=pltpu.CompilerParams(dimension_semantics=("arbitrary",)),
        cost_estimate=pl.CostEstimate(
            flops=flops, transcendentals=SETS * tokens * TILE * heads, bytes_accessed=bytes_accessed
        ),
    )(flags, recv, recv, recv, recv, kv_below, kv_above, kv_left, kv_right)


def shifted(block, axis, distance):
    devices = range(lax.axis_size(axis))
    route = [(i - distance, i) for i in devices if i - distance in devices]
    return lax.ppermute(block, axis, route)


def shards(query_rows, key_rows, value_rows, out_cotangent, tile_slot, window_reach):
    tokens_here, channels = query_rows.shape
    tm_count = lax.axis_size("tm")
    space_count = lax.axis_size("space")
    per_peer = tokens_here // (tm_count * space_count)
    own_rank = lax.axis_index("tm") * space_count + lax.axis_index("space")
    landing = tile_slot // tokens_here * per_peer + tile_slot % tokens_here - own_rank * per_peer
    chosen = (
        jnp.zeros((tokens_here,), jnp.int32)
        .at[landing]
        .set(jnp.arange(tokens_here, dtype=jnp.int32))
    )
    gathered = [rows[chosen] for rows in (query_rows, key_rows, value_rows, out_cotangent)]
    slab_index = lax.axis_index("tm")
    column = lax.axis_index("space")
    own_reach = lax.dynamic_index_in_dim(window_reach, slab_index, 0, keepdims=False)[0]
    flags = jnp.stack(
        [own_reach[0] > 0, own_reach[0] >= 0, own_reach[1] > 0, column > 0, column < space_count - 1]
    ).astype(jnp.int32)
    width = channels // CHUNKS
    backs = []
    for chunk in range(CHUNKS):
        cols = slice(chunk * width, (chunk + 1) * width)
        send = jnp.concatenate([rows[:, cols] for rows in gathered], axis=1)
        recv = lax.all_to_all(send, ("tm", "space"), split_axis=0, concat_axis=0, tiled=True)
        kv_own = jnp.stack([recv[:, width:2 * width], recv[:, 2 * width:3 * width]])
        kv_below = shifted(kv_own, "tm", 1)
        kv_above = shifted(kv_own, "tm", -1)
        kv_left = shifted(kv_own, "space", 1)
        kv_right = shifted(kv_own, "space", -1)
        attended, query_grad, key_own, value_own, nb_b, nb_a, nb_l, nb_r = attend_tile(
            flags, recv, kv_below, kv_above, kv_left, kv_right
        )
        from_above = shifted(nb_b, "tm", -1)
        from_below = shifted(nb_a, "tm", 1)
        from_right = shifted(nb_l, "space", -1)
        from_left = shifted(nb_r, "space", 1)
        terms = (
            from_above.astype(jnp.float32)
            + from_below.astype(jnp.float32)
            + from_right.astype(jnp.float32)
            + from_left.astype(jnp.float32)
        )
        key_grad = (key_own + terms[0]).astype(jnp.bfloat16)
        value_grad = (value_own + terms[1]).astype(jnp.bfloat16)
        out_tile = jnp.concatenate([attended, query_grad, key_grad, value_grad], axis=1)
        backs.append(lax.all_to_all(out_tile, ("tm", "space"), split_axis=0, concat_axis=0, tiled=True))
    back = jnp.concatenate(
        [backs[chunk][:, i * width:(i + 1) * width] for i in range(4) for chunk in range(CHUNKS)], axis=1
    )
    rows = back[landing]
    return tuple(rows[:, i * channels:(i + 1) * channels] for i in range(4))


def solution(mesh):
    return jax.shard_map(
        shards,
        mesh=mesh,
        in_specs=(
            P(("tm", "space"), None),
            P(("tm", "space"), None),
            P(("tm", "space"), None),
            P(("tm", "space"), None),
            P(("tm", "space")),
            P(None, "space", None),
        ),
        out_specs=(
            P(("tm", "space"), None),
            P(("tm", "space"), None),
            P(("tm", "space"), None),
            P(("tm", "space"), None),
        ),
        check_vma=False,
    )
```

```python
import functools

import jax
import jax.numpy as jnp
from jax import lax
from jax.experimental import pallas as pl
from jax.experimental.pallas import tpu as pltpu
from jax.sharding import PartitionSpec as P

H = 20
HD = 128
TILE = 256
SETS = 5
CHUNKS = 2
NT_DIMS = (((1,), (1,)), ((), ()))


def _attn_kernel(flags_ref, q_ref, g_ref, k_ref, v_ref, kb_ref, ka_ref, kl_ref, kr_ref,
                 o_ref, dq_ref, dko_ref, dvo_ref, nb_b, nb_a, nb_l, nb_r, s_scr, dp_scr):
    scale = HD ** (-0.5)
    q = q_ref[...]
    g = g_ref[...]
    keys = [kb_ref[0], k_ref[...], ka_ref[0], kl_ref[0], kr_ref[0]]
    vals = [kb_ref[1], v_ref[...], ka_ref[1], kl_ref[1], kr_ref[1]]
    nb_out = [nb_b, None, nb_a, nb_l, nb_r]
    vis = [flags_ref[a] > 0 for a in range(SETS)]

    m = jnp.full((TILE, 1), -1e30, jnp.float32)
    for a in range(SETS):
        s = lax.dot_general(q, keys[a], NT_DIMS, preferred_element_type=jnp.float32) * scale
        s = jnp.where(vis[a], s, -1e30)
        s_scr[a] = s
        m = jnp.maximum(m, jnp.max(s, axis=1, keepdims=True))
    l = jnp.zeros((TILE, 1), jnp.float32)
    for a in range(SETS):
        e = jnp.where(vis[a], jnp.exp(s_scr[a] - m), 0.0)
        s_scr[a] = e
        l = l + jnp.sum(e, axis=1, keepdims=True)
    inv = 1.0 / l
    o = jnp.zeros((TILE, HD), jnp.float32)
    rd = jnp.zeros((TILE, 1), jnp.float32)
    for a in range(SETS):
        p = s_scr[a] * inv
        pb = p.astype(jnp.bfloat16)
        o = o + jnp.dot(pb, vals[a], preferred_element_type=jnp.float32)
        dp = lax.dot_general(g, vals[a], NT_DIMS, preferred_element_type=jnp.float32)
        rd = rd + jnp.sum(p * dp, axis=1, keepdims=True)
        s_scr[a] = p
        dp_scr[a] = dp
        dv = jnp.dot(p.T.astype(jnp.bfloat16), g, preferred_element_type=jnp.float32)
        if a == 1:
            dvo_ref[...] = dv
        else:
            nb_out[a][1] = dv.astype(jnp.bfloat16)
    o_ref[...] = o.astype(jnp.bfloat16)
    dq = jnp.zeros((TILE, HD), jnp.float32)
    for a in range(SETS):
        ds = s_scr[a] * (dp_scr[a] - rd) * scale
        dq = dq + jnp.dot(ds.astype(jnp.bfloat16), keys[a], preferred_element_type=jnp.float32)
        dk = jnp.dot(ds.T.astype(jnp.bfloat16), q, preferred_element_type=jnp.float32)
        if a == 1:
            dko_ref[...] = dk
        else:
            nb_out[a][0] = dk.astype(jnp.bfloat16)
    dq_ref[...] = dq.astype(jnp.bfloat16)


def attend_tile(flags, recv, kv_below, kv_above, kv_left, kv_right):
    tokens = recv.shape[0]
    heads = recv.shape[1] // (4 * HD)
    own = lambda part: pl.BlockSpec((tokens, HD), lambda h, f, part=part: (0, part * heads + h))
    pair = pl.BlockSpec((2, tokens, HD), lambda h, f: (0, 0, h))
    head = pl.BlockSpec((tokens, HD), lambda h, f: (0, h))
    flops = 6 * SETS * 2 * tokens * TILE * HD * heads
    bytes_accessed = (4 * 2 + 4 * 4 + 4 * 2 * 2 + 2 * 2 + 2 * 4 + 4 * 2 * 2) * tokens * HD * heads
    out_shape = (
        jax.ShapeDtypeStruct((tokens, heads * HD), jnp.bfloat16),
        jax.ShapeDtypeStruct((tokens, heads * HD), jnp.bfloat16),
        jax.ShapeDtypeStruct((tokens, heads * HD), jnp.float32),
        jax.ShapeDtypeStruct((tokens, heads * HD), jnp.float32),
    ) + tuple(jax.ShapeDtypeStruct((2, tokens, heads * HD), jnp.bfloat16) for _ in range(4))
    return pl.pallas_call(
        _attn_kernel,
        out_shape=out_shape,
        grid_spec=pltpu.PrefetchScalarGridSpec(
            num_scalar_prefetch=1,
            grid=(heads,),
            in_specs=[own(0), own(3), own(1), own(2), pair, pair, pair, pair],
            out_specs=[head, head, head, head, pair, pair, pair, pair],
            scratch_shapes=[
                pltpu.VMEM((SETS, tokens, TILE), jnp.float32),
                pltpu.VMEM((SETS, tokens, TILE), jnp.float32),
            ],
        ),
        compiler_params=pltpu.CompilerParams(dimension_semantics=("arbitrary",)),
        cost_estimate=pl.CostEstimate(
            flops=flops, transcendentals=SETS * tokens * TILE * heads, bytes_accessed=bytes_accessed
        ),
    )(flags, recv, recv, recv, recv, kv_below, kv_above, kv_left, kv_right)


def shifted(block, axis, distance):
    devices = range(lax.axis_size(axis))
    route = [(i - distance, i) for i in devices if i - distance in devices]
    return lax.ppermute(block, axis, route)


def shards(query_rows, key_rows, value_rows, out_cotangent, tile_slot, window_reach):
    tokens_here, channels = query_rows.shape
    tm_count = lax.axis_size("tm")
    space_count = lax.axis_size("space")
    per_peer = tokens_here // (tm_count * space_count)
    own_rank = lax.axis_index("tm") * space_count + lax.axis_index("space")
    landing = tile_slot // tokens_here * per_peer + tile_slot % tokens_here - own_rank * per_peer
    chosen = (
        jnp.zeros((tokens_here,), jnp.int32)
        .at[landing]
        .set(jnp.arange(tokens_here, dtype=jnp.int32))
    )
    gathered = [rows[chosen] for rows in (query_rows, key_rows, value_rows, out_cotangent)]
    slab_index = lax.axis_index("tm")
    column = lax.axis_index("space")
    own_reach = lax.dynamic_index_in_dim(window_reach, slab_index, 0, keepdims=False)[0]
    flags = jnp.stack(
        [own_reach[0] > 0, own_reach[0] >= 0, own_reach[1] > 0, column > 0, column < space_count - 1]
    ).astype(jnp.int32)
    width = channels // CHUNKS
    backs = []
    gate = None
    for chunk in range(CHUNKS):
        cols = slice(chunk * width, (chunk + 1) * width)
        send = jnp.concatenate([rows[:, cols] for rows in gathered], axis=1)
        recv = lax.all_to_all(send, ("tm", "space"), split_axis=0, concat_axis=0, tiled=True)
        kv_own = jnp.stack([recv[:, width:2 * width], recv[:, 2 * width:3 * width]])
        if gate is not None:
            kv_own = lax.optimization_barrier((kv_own,) + gate)[0]
        halo = (
            shifted(kv_own, "tm", 1),
            shifted(kv_own, "tm", -1),
            shifted(kv_own, "space", 1),
            shifted(kv_own, "space", -1),
        )
        attended, query_grad, key_own, value_own, nb_b, nb_a, nb_l, nb_r = attend_tile(
            flags, recv, *halo
        )
        gate = halo
        backs.append((attended, query_grad, key_own, value_own, nb_b, nb_a, nb_l, nb_r))
    outs = []
    prior = None
    for chunk in range(CHUNKS):
        attended, query_grad, key_own, value_own, nb_b, nb_a, nb_l, nb_r = backs[chunk]
        sends = (nb_b, nb_a, nb_l, nb_r)
        if prior is not None:
            sends = lax.optimization_barrier(sends + prior)[:4]
        elif CHUNKS > 1:
            sends = lax.optimization_barrier(sends + gate)[:4]
        nb_b, nb_a, nb_l, nb_r = sends
        received = (
            shifted(nb_b, "tm", -1),
            shifted(nb_a, "tm", 1),
            shifted(nb_l, "space", -1),
            shifted(nb_r, "space", 1),
        )
        prior = received
        terms = sum(part.astype(jnp.float32) for part in received)
        key_grad = (key_own + terms[0]).astype(jnp.bfloat16)
        value_grad = (value_own + terms[1]).astype(jnp.bfloat16)
        out_tile = jnp.concatenate([attended, query_grad, key_grad, value_grad], axis=1)
        outs.append(lax.all_to_all(out_tile, ("tm", "space"), split_axis=0, concat_axis=0, tiled=True))
    return tuple(
        jnp.concatenate([outs[chunk][:, i * width:(i + 1) * width] for chunk in range(CHUNKS)], axis=1)[landing]
        for i in range(4)
    )


def solution(mesh):
    return jax.shard_map(
        shards,
        mesh=mesh,
        in_specs=(
            P(("tm", "space"), None),
            P(("tm", "space"), None),
            P(("tm", "space"), None),
            P(("tm", "space"), None),
            P(("tm", "space")),
            P(None, "space", None),
        ),
        out_specs=(
            P(("tm", "space"), None),
            P(("tm", "space"), None),
            P(("tm", "space"), None),
            P(("tm", "space"), None),
        ),
        check_vma=False,
    )
```

```python
import functools

import jax
import jax.numpy as jnp
from jax import lax
from jax.experimental import pallas as pl
from jax.experimental.pallas import tpu as pltpu
from jax.sharding import PartitionSpec as P

H = 20
HD = 128
TILE = 256
SETS = 5
CHUNKS = 4
NT_DIMS = (((1,), (1,)), ((), ()))


def _attn_kernel(flags_ref, q_ref, g_ref, k_ref, v_ref, kb_ref, ka_ref, kl_ref, kr_ref,
                 o_ref, dq_ref, dko_ref, dvo_ref, nb_b, nb_a, nb_l, nb_r, s_scr, dp_scr):
    scale = HD ** (-0.5)
    q = q_ref[...]
    g = g_ref[...]
    keys = [kb_ref[0], k_ref[...], ka_ref[0], kl_ref[0], kr_ref[0]]
    vals = [kb_ref[1], v_ref[...], ka_ref[1], kl_ref[1], kr_ref[1]]
    nb_out = [nb_b, None, nb_a, nb_l, nb_r]
    vis = [flags_ref[a] > 0 for a in range(SETS)]

    m = jnp.full((TILE, 1), -1e30, jnp.float32)
    for a in range(SETS):
        s = lax.dot_general(q, keys[a], NT_DIMS, preferred_element_type=jnp.float32) * scale
        s = jnp.where(vis[a], s, -1e30)
        s_scr[a] = s
        m = jnp.maximum(m, jnp.max(s, axis=1, keepdims=True))
    l = jnp.zeros((TILE, 1), jnp.float32)
    for a in range(SETS):
        e = jnp.where(vis[a], jnp.exp(s_scr[a] - m), 0.0)
        s_scr[a] = e
        l = l + jnp.sum(e, axis=1, keepdims=True)
    inv = 1.0 / l
    o = jnp.zeros((TILE, HD), jnp.float32)
    rd = jnp.zeros((TILE, 1), jnp.float32)
    for a in range(SETS):
        p = s_scr[a] * inv
        pb = p.astype(jnp.bfloat16)
        o = o + jnp.dot(pb, vals[a], preferred_element_type=jnp.float32)
        dp = lax.dot_general(g, vals[a], NT_DIMS, preferred_element_type=jnp.float32)
        rd = rd + jnp.sum(p * dp, axis=1, keepdims=True)
        s_scr[a] = p
        dp_scr[a] = dp
        dv = jnp.dot(p.T.astype(jnp.bfloat16), g, preferred_element_type=jnp.float32)
        if a == 1:
            dvo_ref[...] = dv
        else:
            nb_out[a][1] = dv.astype(jnp.bfloat16)
    o_ref[...] = o.astype(jnp.bfloat16)
    dq = jnp.zeros((TILE, HD), jnp.float32)
    for a in range(SETS):
        ds = s_scr[a] * (dp_scr[a] - rd) * scale
        dq = dq + jnp.dot(ds.astype(jnp.bfloat16), keys[a], preferred_element_type=jnp.float32)
        dk = jnp.dot(ds.T.astype(jnp.bfloat16), q, preferred_element_type=jnp.float32)
        if a == 1:
            dko_ref[...] = dk
        else:
            nb_out[a][0] = dk.astype(jnp.bfloat16)
    dq_ref[...] = dq.astype(jnp.bfloat16)


def attend_tile(flags, recv, kv_below, kv_above, kv_left, kv_right):
    tokens = recv.shape[0]
    heads = recv.shape[1] // (4 * HD)
    own = lambda part: pl.BlockSpec((tokens, HD), lambda h, f, part=part: (0, part * heads + h))
    pair = pl.BlockSpec((2, tokens, HD), lambda h, f: (0, 0, h))
    head = pl.BlockSpec((tokens, HD), lambda h, f: (0, h))
    flops = 6 * SETS * 2 * tokens * TILE * HD * heads
    bytes_accessed = (4 * 2 + 4 * 4 + 4 * 2 * 2 + 2 * 2 + 2 * 4 + 4 * 2 * 2) * tokens * HD * heads
    out_shape = (
        jax.ShapeDtypeStruct((tokens, heads * HD), jnp.bfloat16),
        jax.ShapeDtypeStruct((tokens, heads * HD), jnp.bfloat16),
        jax.ShapeDtypeStruct((tokens, heads * HD), jnp.float32),
        jax.ShapeDtypeStruct((tokens, heads * HD), jnp.float32),
    ) + tuple(jax.ShapeDtypeStruct((2, tokens, heads * HD), jnp.bfloat16) for _ in range(4))
    return pl.pallas_call(
        _attn_kernel,
        out_shape=out_shape,
        grid_spec=pltpu.PrefetchScalarGridSpec(
            num_scalar_prefetch=1,
            grid=(heads,),
            in_specs=[own(0), own(3), own(1), own(2), pair, pair, pair, pair],
            out_specs=[head, head, head, head, pair, pair, pair, pair],
            scratch_shapes=[
                pltpu.VMEM((SETS, tokens, TILE), jnp.float32),
                pltpu.VMEM((SETS, tokens, TILE), jnp.float32),
            ],
        ),
        compiler_params=pltpu.CompilerParams(dimension_semantics=("arbitrary",)),
        cost_estimate=pl.CostEstimate(
            flops=flops, transcendentals=SETS * tokens * TILE * heads, bytes_accessed=bytes_accessed
        ),
    )(flags, recv, recv, recv, recv, kv_below, kv_above, kv_left, kv_right)


def shifted(block, axis, distance):
    devices = range(lax.axis_size(axis))
    route = [(i - distance, i) for i in devices if i - distance in devices]
    return lax.ppermute(block, axis, route)


def shards(query_rows, key_rows, value_rows, out_cotangent, tile_slot, window_reach):
    tokens_here, channels = query_rows.shape
    tm_count = lax.axis_size("tm")
    space_count = lax.axis_size("space")
    per_peer = tokens_here // (tm_count * space_count)
    own_rank = lax.axis_index("tm") * space_count + lax.axis_index("space")
    landing = tile_slot // tokens_here * per_peer + tile_slot % tokens_here - own_rank * per_peer
    chosen = (
        jnp.zeros((tokens_here,), jnp.int32)
        .at[landing]
        .set(jnp.arange(tokens_here, dtype=jnp.int32))
    )
    gathered = [rows[chosen] for rows in (query_rows, key_rows, value_rows, out_cotangent)]
    slab_index = lax.axis_index("tm")
    column = lax.axis_index("space")
    own_reach = lax.dynamic_index_in_dim(window_reach, slab_index, 0, keepdims=False)[0]
    flags = jnp.stack(
        [own_reach[0] > 0, own_reach[0] >= 0, own_reach[1] > 0, column > 0, column < space_count - 1]
    ).astype(jnp.int32)
    width = channels // CHUNKS
    backs = []
    gate = None
    for chunk in range(CHUNKS):
        cols = slice(chunk * width, (chunk + 1) * width)
        send = jnp.concatenate([rows[:, cols] for rows in gathered], axis=1)
        recv = lax.all_to_all(send, ("tm", "space"), split_axis=0, concat_axis=0, tiled=True)
        kv_own = jnp.stack([recv[:, width:2 * width], recv[:, 2 * width:3 * width]])
        if gate is not None:
            kv_own = lax.optimization_barrier((kv_own,) + gate)[0]
        halo = (
            shifted(kv_own, "tm", 1),
            shifted(kv_own, "tm", -1),
            shifted(kv_own, "space", 1),
            shifted(kv_own, "space", -1),
        )
        attended, query_grad, key_own, value_own, nb_b, nb_a, nb_l, nb_r = attend_tile(
            flags, recv, *halo
        )
        gate = halo
        backs.append((attended, query_grad, key_own, value_own, nb_b, nb_a, nb_l, nb_r))
    outs = []
    prior = None
    for chunk in range(CHUNKS):
        attended, query_grad, key_own, value_own, nb_b, nb_a, nb_l, nb_r = backs[chunk]
        sends = (nb_b, nb_a, nb_l, nb_r)
        if prior is not None:
            sends = lax.optimization_barrier(sends + prior)[:4]
        elif CHUNKS > 1:
            sends = lax.optimization_barrier(sends + gate)[:4]
        nb_b, nb_a, nb_l, nb_r = sends
        received = (
            shifted(nb_b, "tm", -1),
            shifted(nb_a, "tm", 1),
            shifted(nb_l, "space", -1),
            shifted(nb_r, "space", 1),
        )
        prior = received
        terms = sum(part.astype(jnp.float32) for part in received)
        key_grad = (key_own + terms[0]).astype(jnp.bfloat16)
        value_grad = (value_own + terms[1]).astype(jnp.bfloat16)
        out_tile = jnp.concatenate([attended, query_grad, key_grad, value_grad], axis=1)
        outs.append(lax.all_to_all(out_tile, ("tm", "space"), split_axis=0, concat_axis=0, tiled=True))
    return tuple(
        jnp.concatenate([outs[chunk][:, i * width:(i + 1) * width] for chunk in range(CHUNKS)], axis=1)[landing]
        for i in range(4)
    )


def solution(mesh):
    return jax.shard_map(
        shards,
        mesh=mesh,
        in_specs=(
            P(("tm", "space"), None),
            P(("tm", "space"), None),
            P(("tm", "space"), None),
            P(("tm", "space"), None),
            P(("tm", "space")),
            P(None, "space", None),
        ),
        out_specs=(
            P(("tm", "space"), None),
            P(("tm", "space"), None),
            P(("tm", "space"), None),
            P(("tm", "space"), None),
        ),
        check_vma=False,
    )
```

```python
import functools

import jax
import jax.numpy as jnp
from jax import lax
from jax.experimental import pallas as pl
from jax.experimental.pallas import tpu as pltpu
from jax.sharding import PartitionSpec as P

H = 20
HD = 128
TILE = 256
SETS = 5
CHUNKS = 2
NT_DIMS = (((1,), (1,)), ((), ()))


def _attn_kernel(flags_ref, q_ref, g_ref, k_ref, v_ref, kb_ref, ka_ref, kl_ref, kr_ref,
                 o_ref, dq_ref, dko_ref, dvo_ref, nb_b, nb_a, nb_l, nb_r, s_scr, dp_scr):
    scale = HD ** (-0.5)
    q = q_ref[...]
    g = g_ref[...]
    keys = [kb_ref[0], k_ref[...], ka_ref[0], kl_ref[0], kr_ref[0]]
    vals = [kb_ref[1], v_ref[...], ka_ref[1], kl_ref[1], kr_ref[1]]
    nb_out = [nb_b, None, nb_a, nb_l, nb_r]
    vis = [flags_ref[a] > 0 for a in range(SETS)]

    m = jnp.full((TILE, 1), -1e30, jnp.float32)
    for a in range(SETS):
        s = lax.dot_general(q, keys[a], NT_DIMS, preferred_element_type=jnp.float32) * scale
        s = jnp.where(vis[a], s, -1e30)
        s_scr[a] = s
        m = jnp.maximum(m, jnp.max(s, axis=1, keepdims=True))
    l = jnp.zeros((TILE, 1), jnp.float32)
    for a in range(SETS):
        e = jnp.where(vis[a], jnp.exp(s_scr[a] - m), 0.0)
        s_scr[a] = e
        l = l + jnp.sum(e, axis=1, keepdims=True)
    inv = 1.0 / l
    o = jnp.zeros((TILE, HD), jnp.float32)
    rd = jnp.zeros((TILE, 1), jnp.float32)
    for a in range(SETS):
        p = s_scr[a] * inv
        pb = p.astype(jnp.bfloat16)
        o = o + jnp.dot(pb, vals[a], preferred_element_type=jnp.float32)
        dp = lax.dot_general(g, vals[a], NT_DIMS, preferred_element_type=jnp.float32)
        rd = rd + jnp.sum(p * dp, axis=1, keepdims=True)
        s_scr[a] = p
        dp_scr[a] = dp
        dv = jnp.dot(p.T.astype(jnp.bfloat16), g, preferred_element_type=jnp.float32)
        if a == 1:
            dvo_ref[...] = dv
        else:
            nb_out[a][1] = dv.astype(jnp.bfloat16)
    o_ref[...] = o.astype(jnp.bfloat16)
    dq = jnp.zeros((TILE, HD), jnp.float32)
    for a in range(SETS):
        ds = s_scr[a] * (dp_scr[a] - rd) * scale
        dq = dq + jnp.dot(ds.astype(jnp.bfloat16), keys[a], preferred_element_type=jnp.float32)
        dk = jnp.dot(ds.T.astype(jnp.bfloat16), q, preferred_element_type=jnp.float32)
        if a == 1:
            dko_ref[...] = dk
        else:
            nb_out[a][0] = dk.astype(jnp.bfloat16)
    dq_ref[...] = dq.astype(jnp.bfloat16)


def attend_tile(flags, recv, kv_below, kv_above, kv_left, kv_right):
    tokens = recv.shape[0]
    heads = recv.shape[1] // (4 * HD)
    own = lambda part: pl.BlockSpec((tokens, HD), lambda h, f, part=part: (0, part * heads + h))
    pair = pl.BlockSpec((2, tokens, HD), lambda h, f: (0, 0, h))
    head = pl.BlockSpec((tokens, HD), lambda h, f: (0, h))
    flops = 6 * SETS * 2 * tokens * TILE * HD * heads
    bytes_accessed = (4 * 2 + 4 * 4 + 4 * 2 * 2 + 2 * 2 + 2 * 4 + 4 * 2 * 2) * tokens * HD * heads
    out_shape = (
        jax.ShapeDtypeStruct((tokens, heads * HD), jnp.bfloat16),
        jax.ShapeDtypeStruct((tokens, heads * HD), jnp.bfloat16),
        jax.ShapeDtypeStruct((tokens, heads * HD), jnp.float32),
        jax.ShapeDtypeStruct((tokens, heads * HD), jnp.float32),
    ) + tuple(jax.ShapeDtypeStruct((2, tokens, heads * HD), jnp.bfloat16) for _ in range(4))
    return pl.pallas_call(
        _attn_kernel,
        out_shape=out_shape,
        grid_spec=pltpu.PrefetchScalarGridSpec(
            num_scalar_prefetch=1,
            grid=(heads,),
            in_specs=[own(0), own(3), own(1), own(2), pair, pair, pair, pair],
            out_specs=[head, head, head, head, pair, pair, pair, pair],
            scratch_shapes=[
                pltpu.VMEM((SETS, tokens, TILE), jnp.float32),
                pltpu.VMEM((SETS, tokens, TILE), jnp.float32),
            ],
        ),
        compiler_params=pltpu.CompilerParams(dimension_semantics=("arbitrary",)),
        cost_estimate=pl.CostEstimate(
            flops=flops, transcendentals=SETS * tokens * TILE * heads, bytes_accessed=bytes_accessed
        ),
    )(flags, recv, recv, recv, recv, kv_below, kv_above, kv_left, kv_right)


def shifted(block, axis, distance):
    devices = range(lax.axis_size(axis))
    route = [(i - distance, i) for i in devices if i - distance in devices]
    return lax.ppermute(block, axis, route)


def shards(query_rows, key_rows, value_rows, out_cotangent, tile_slot, window_reach):
    tokens_here, channels = query_rows.shape
    tm_count = lax.axis_size("tm")
    space_count = lax.axis_size("space")
    per_peer = tokens_here // (tm_count * space_count)
    own_rank = lax.axis_index("tm") * space_count + lax.axis_index("space")
    landing = tile_slot // tokens_here * per_peer + tile_slot % tokens_here - own_rank * per_peer
    chosen = (
        jnp.zeros((tokens_here,), jnp.int32)
        .at[landing]
        .set(jnp.arange(tokens_here, dtype=jnp.int32))
    )
    gathered = [rows[chosen] for rows in (query_rows, key_rows, value_rows, out_cotangent)]
    slab_index = lax.axis_index("tm")
    column = lax.axis_index("space")
    own_reach = lax.dynamic_index_in_dim(window_reach, slab_index, 0, keepdims=False)[0]
    flags = jnp.stack(
        [own_reach[0] > 0, own_reach[0] >= 0, own_reach[1] > 0, column > 0, column < space_count - 1]
    ).astype(jnp.int32)
    width = channels // CHUNKS
    backs = []
    gate = None
    for chunk in range(CHUNKS):
        cols = slice(chunk * width, (chunk + 1) * width)
        send = jnp.concatenate([rows[:, cols] for rows in gathered], axis=1)
        recv = lax.all_to_all(send, ("tm", "space"), split_axis=0, concat_axis=0, tiled=True)
        kv_own = jnp.stack([recv[:, width:2 * width], recv[:, 2 * width:3 * width]])
        if gate is not None:
            kv_own = lax.optimization_barrier((kv_own,) + gate)[0]
        halo = (
            shifted(kv_own, "tm", 1),
            shifted(kv_own, "tm", -1),
            shifted(kv_own, "space", 1),
            shifted(kv_own, "space", -1),
        )
        attended, query_grad, key_own, value_own, nb_b, nb_a, nb_l, nb_r = attend_tile(
            flags, recv, *halo
        )
        gate = halo
        early = jnp.concatenate([attended, query_grad], axis=1)
        early = lax.all_to_all(early, ("tm", "space"), split_axis=0, concat_axis=0, tiled=True)
        backs.append((early, key_own, value_own, nb_b, nb_a, nb_l, nb_r))
    outs = []
    prior = None
    for chunk in range(CHUNKS):
        early, key_own, value_own, nb_b, nb_a, nb_l, nb_r = backs[chunk]
        sends = (nb_b, nb_a, nb_l, nb_r)
        if prior is not None:
            sends = lax.optimization_barrier(sends + prior)[:4]
        elif CHUNKS > 1:
            sends = lax.optimization_barrier(sends + gate)[:4]
        nb_b, nb_a, nb_l, nb_r = sends
        received = (
            shifted(nb_b, "tm", -1),
            shifted(nb_a, "tm", 1),
            shifted(nb_l, "space", -1),
            shifted(nb_r, "space", 1),
        )
        prior = received
        terms = sum(part.astype(jnp.float32) for part in received)
        key_grad = (key_own + terms[0]).astype(jnp.bfloat16)
        value_grad = (value_own + terms[1]).astype(jnp.bfloat16)
        late = jnp.concatenate([key_grad, value_grad], axis=1)
        late = lax.all_to_all(late, ("tm", "space"), split_axis=0, concat_axis=0, tiled=True)
        outs.append(jnp.concatenate([early, late], axis=1))
    return tuple(
        jnp.concatenate([outs[chunk][:, i * width:(i + 1) * width] for chunk in range(CHUNKS)], axis=1)[landing]
        for i in range(4)
    )


def solution(mesh):
    return jax.shard_map(
        shards,
        mesh=mesh,
        in_specs=(
            P(("tm", "space"), None),
            P(("tm", "space"), None),
            P(("tm", "space"), None),
            P(("tm", "space"), None),
            P(("tm", "space")),
            P(None, "space", None),
        ),
        out_specs=(
            P(("tm", "space"), None),
            P(("tm", "space"), None),
            P(("tm", "space"), None),
            P(("tm", "space"), None),
        ),
        check_vma=False,
    )
```

```python
import functools

import jax
import jax.numpy as jnp
from jax import lax
from jax.experimental import pallas as pl
from jax.experimental.pallas import tpu as pltpu
from jax.sharding import PartitionSpec as P

H = 20
HD = 128
TILE = 256
SETS = 5
CHUNKS = 2
NT_DIMS = (((1,), (1,)), ((), ()))


def _attn_kernel(flags_ref, q_ref, g_ref, k_ref, v_ref, kb_ref, ka_ref, kl_ref, kr_ref,
                 o_ref, dq_ref, dko_ref, dvo_ref, nb_b, nb_a, nb_l, nb_r, s_scr, dp_scr):
    scale = HD ** (-0.5)
    q = q_ref[...]
    g = g_ref[...]
    keys = [kb_ref[0], k_ref[...], ka_ref[0], kl_ref[0], kr_ref[0]]
    vals = [kb_ref[1], v_ref[...], ka_ref[1], kl_ref[1], kr_ref[1]]
    nb_out = [nb_b, None, nb_a, nb_l, nb_r]
    vis = [flags_ref[a] > 0 for a in range(SETS)]

    m = jnp.full((TILE, 1), -1e30, jnp.float32)
    for a in range(SETS):
        s = lax.dot_general(q, keys[a], NT_DIMS, preferred_element_type=jnp.float32) * scale
        s = jnp.where(vis[a], s, -1e30)
        s_scr[a] = s
        m = jnp.maximum(m, jnp.max(s, axis=1, keepdims=True))
    l = jnp.zeros((TILE, 1), jnp.float32)
    for a in range(SETS):
        e = jnp.where(vis[a], jnp.exp(s_scr[a] - m), 0.0)
        s_scr[a] = e
        l = l + jnp.sum(e, axis=1, keepdims=True)
    inv = 1.0 / l
    o = jnp.zeros((TILE, HD), jnp.float32)
    rd = jnp.zeros((TILE, 1), jnp.float32)
    for a in range(SETS):
        p = s_scr[a] * inv
        pb = p.astype(jnp.bfloat16)
        o = o + jnp.dot(pb, vals[a], preferred_element_type=jnp.float32)
        dp = lax.dot_general(g, vals[a], NT_DIMS, preferred_element_type=jnp.float32)
        rd = rd + jnp.sum(p * dp, axis=1, keepdims=True)
        s_scr[a] = p
        dp_scr[a] = dp
        dv = jnp.dot(p.T.astype(jnp.bfloat16), g, preferred_element_type=jnp.float32)
        if a == 1:
            dvo_ref[...] = dv
        else:
            nb_out[a][1] = dv.astype(jnp.bfloat16)
    o_ref[...] = o.astype(jnp.bfloat16)
    dq = jnp.zeros((TILE, HD), jnp.float32)
    for a in range(SETS):
        ds = s_scr[a] * (dp_scr[a] - rd) * scale
        dq = dq + jnp.dot(ds.astype(jnp.bfloat16), keys[a], preferred_element_type=jnp.float32)
        dk = jnp.dot(ds.T.astype(jnp.bfloat16), q, preferred_element_type=jnp.float32)
        if a == 1:
            dko_ref[...] = dk
        else:
            nb_out[a][0] = dk.astype(jnp.bfloat16)
    dq_ref[...] = dq.astype(jnp.bfloat16)


def attend_tile(flags, qg, kv, kv_below, kv_above, kv_left, kv_right):
    tokens = qg.shape[0]
    heads = qg.shape[1] // (2 * HD)
    own = lambda part: pl.BlockSpec((tokens, HD), lambda h, f, part=part: (0, part * heads + h))
    pair = pl.BlockSpec((2, tokens, HD), lambda h, f: (0, 0, h))
    head = pl.BlockSpec((tokens, HD), lambda h, f: (0, h))
    flops = 6 * SETS * 2 * tokens * TILE * HD * heads
    bytes_accessed = (4 * 2 + 4 * 4 + 4 * 2 * 2 + 2 * 2 + 2 * 4 + 4 * 2 * 2) * tokens * HD * heads
    out_shape = (
        jax.ShapeDtypeStruct((tokens, heads * HD), jnp.bfloat16),
        jax.ShapeDtypeStruct((tokens, heads * HD), jnp.bfloat16),
        jax.ShapeDtypeStruct((tokens, heads * HD), jnp.float32),
        jax.ShapeDtypeStruct((tokens, heads * HD), jnp.float32),
    ) + tuple(jax.ShapeDtypeStruct((2, tokens, heads * HD), jnp.bfloat16) for _ in range(4))
    return pl.pallas_call(
        _attn_kernel,
        out_shape=out_shape,
        grid_spec=pltpu.PrefetchScalarGridSpec(
            num_scalar_prefetch=1,
            grid=(heads,),
            in_specs=[own(0), own(1), own(0), own(1), pair, pair, pair, pair],
            out_specs=[head, head, head, head, pair, pair, pair, pair],
            scratch_shapes=[
                pltpu.VMEM((SETS, tokens, TILE), jnp.float32),
                pltpu.VMEM((SETS, tokens, TILE), jnp.float32),
            ],
        ),
        compiler_params=pltpu.CompilerParams(dimension_semantics=("arbitrary",)),
        cost_estimate=pl.CostEstimate(
            flops=flops, transcendentals=SETS * tokens * TILE * heads, bytes_accessed=bytes_accessed
        ),
    )(flags, qg, qg, kv, kv, kv_below, kv_above, kv_left, kv_right)


def shifted(block, axis, distance):
    devices = range(lax.axis_size(axis))
    route = [(i - distance, i) for i in devices if i - distance in devices]
    return lax.ppermute(block, axis, route)


def shards(query_rows, key_rows, value_rows, out_cotangent, tile_slot, window_reach):
    tokens_here, channels = query_rows.shape
    tm_count = lax.axis_size("tm")
    space_count = lax.axis_size("space")
    per_peer = tokens_here // (tm_count * space_count)
    own_rank = lax.axis_index("tm") * space_count + lax.axis_index("space")
    landing = tile_slot // tokens_here * per_peer + tile_slot % tokens_here - own_rank * per_peer
    chosen = (
        jnp.zeros((tokens_here,), jnp.int32)
        .at[landing]
        .set(jnp.arange(tokens_here, dtype=jnp.int32))
    )
    gathered = [rows[chosen] for rows in (query_rows, key_rows, value_rows, out_cotangent)]
    slab_index = lax.axis_index("tm")
    column = lax.axis_index("space")
    own_reach = lax.dynamic_index_in_dim(window_reach, slab_index, 0, keepdims=False)[0]
    flags = jnp.stack(
        [own_reach[0] > 0, own_reach[0] >= 0, own_reach[1] > 0, column > 0, column < space_count - 1]
    ).astype(jnp.int32)
    width = channels // CHUNKS
    backs = []
    gate = None
    for chunk in range(CHUNKS):
        cols = slice(chunk * width, (chunk + 1) * width)
        send_kv = jnp.concatenate([gathered[1][:, cols], gathered[2][:, cols]], axis=1)
        kv = lax.all_to_all(send_kv, ("tm", "space"), split_axis=0, concat_axis=0, tiled=True)
        kv_own = jnp.stack([kv[:, :width], kv[:, width:]])
        if gate is not None:
            kv_own = lax.optimization_barrier((kv_own,) + gate)[0]
        halo = (
            shifted(kv_own, "tm", 1),
            shifted(kv_own, "tm", -1),
            shifted(kv_own, "space", 1),
            shifted(kv_own, "space", -1),
        )
        send_qg = jnp.concatenate([gathered[0][:, cols], gathered[3][:, cols]], axis=1)
        qg = lax.all_to_all(send_qg, ("tm", "space"), split_axis=0, concat_axis=0, tiled=True)
        attended, query_grad, key_own, value_own, nb_b, nb_a, nb_l, nb_r = attend_tile(
            flags, qg, kv, *halo
        )
        gate = halo
        early = jnp.concatenate([attended, query_grad], axis=1)
        early = lax.all_to_all(early, ("tm", "space"), split_axis=0, concat_axis=0, tiled=True)
        backs.append((early, key_own, value_own, nb_b, nb_a, nb_l, nb_r))
    outs = []
    prior = None
    for chunk in range(CHUNKS):
        early, key_own, value_own, nb_b, nb_a, nb_l, nb_r = backs[chunk]
        sends = (nb_b, nb_a, nb_l, nb_r)
        if prior is not None:
            sends = lax.optimization_barrier(sends + prior)[:4]
        elif CHUNKS > 1:
            sends = lax.optimization_barrier(sends + gate)[:4]
        nb_b, nb_a, nb_l, nb_r = sends
        received = (
            shifted(nb_b, "tm", -1),
            shifted(nb_a, "tm", 1),
            shifted(nb_l, "space", -1),
            shifted(nb_r, "space", 1),
        )
        prior = received
        terms = sum(part.astype(jnp.float32) for part in received)
        key_grad = (key_own + terms[0]).astype(jnp.bfloat16)
        value_grad = (value_own + terms[1]).astype(jnp.bfloat16)
        late = jnp.concatenate([key_grad, value_grad], axis=1)
        late = lax.all_to_all(late, ("tm", "space"), split_axis=0, concat_axis=0, tiled=True)
        outs.append(jnp.concatenate([early, late], axis=1))
    return tuple(
        jnp.concatenate([outs[chunk][:, i * width:(i + 1) * width] for chunk in range(CHUNKS)], axis=1)[landing]
        for i in range(4)
    )


def solution(mesh):
    return jax.shard_map(
        shards,
        mesh=mesh,
        in_specs=(
            P(("tm", "space"), None),
            P(("tm", "space"), None),
            P(("tm", "space"), None),
            P(("tm", "space"), None),
            P(("tm", "space")),
            P(None, "space", None),
        ),
        out_specs=(
            P(("tm", "space"), None),
            P(("tm", "space"), None),
            P(("tm", "space"), None),
            P(("tm", "space"), None),
        ),
        check_vma=False,
    )
```

```python
import functools

import jax
import jax.numpy as jnp
from jax import lax
from jax.experimental import pallas as pl
from jax.experimental.pallas import tpu as pltpu
from jax.sharding import PartitionSpec as P

H = 20
HD = 128
TILE = 256
SETS = 5
CHUNKS = 2
NT_DIMS = (((1,), (1,)), ((), ()))


def _attn_kernel(flags_ref, q_ref, g_ref, k_ref, v_ref, kb_ref, ka_ref, kl_ref, kr_ref,
                 o_ref, dq_ref, dko_ref, dvo_ref, nb_b, nb_a, nb_l, nb_r, s_scr, dp_scr):
    scale = HD ** (-0.5)
    q = q_ref[...]
    g = g_ref[...]
    keys = [kb_ref[0], k_ref[...], ka_ref[0], kl_ref[0], kr_ref[0]]
    vals = [kb_ref[1], v_ref[...], ka_ref[1], kl_ref[1], kr_ref[1]]
    nb_out = [nb_b, None, nb_a, nb_l, nb_r]
    vis = [flags_ref[a] > 0 for a in range(SETS)]

    m = jnp.full((TILE, 1), -1e30, jnp.float32)
    for a in range(SETS):
        s = lax.dot_general(q, keys[a], NT_DIMS, preferred_element_type=jnp.float32) * scale
        s = jnp.where(vis[a], s, -1e30)
        s_scr[a] = s
        m = jnp.maximum(m, jnp.max(s, axis=1, keepdims=True))
    l = jnp.zeros((TILE, 1), jnp.float32)
    for a in range(SETS):
        e = jnp.where(vis[a], jnp.exp(s_scr[a] - m), 0.0)
        s_scr[a] = e
        l = l + jnp.sum(e, axis=1, keepdims=True)
    inv = 1.0 / l
    o = jnp.zeros((TILE, HD), jnp.float32)
    rd = jnp.zeros((TILE, 1), jnp.float32)
    for a in range(SETS):
        p = s_scr[a] * inv
        pb = p.astype(jnp.bfloat16)
        o = o + jnp.dot(pb, vals[a], preferred_element_type=jnp.float32)
        dp = lax.dot_general(g, vals[a], NT_DIMS, preferred_element_type=jnp.float32)
        rd = rd + jnp.sum(p * dp, axis=1, keepdims=True)
        s_scr[a] = p
        dp_scr[a] = dp
        dv = jnp.dot(p.T.astype(jnp.bfloat16), g, preferred_element_type=jnp.float32)
        if a == 1:
            dvo_ref[...] = dv
        else:
            nb_out[a][1] = dv.astype(jnp.bfloat16)
    o_ref[...] = o.astype(jnp.bfloat16)
    dq = jnp.zeros((TILE, HD), jnp.float32)
    for a in range(SETS):
        ds = s_scr[a] * (dp_scr[a] - rd) * scale
        dq = dq + jnp.dot(ds.astype(jnp.bfloat16), keys[a], preferred_element_type=jnp.float32)
        dk = jnp.dot(ds.T.astype(jnp.bfloat16), q, preferred_element_type=jnp.float32)
        if a == 1:
            dko_ref[...] = dk
        else:
            nb_out[a][0] = dk.astype(jnp.bfloat16)
    dq_ref[...] = dq.astype(jnp.bfloat16)


def attend_tile(flags, recv, kv_below, kv_above, kv_left, kv_right):
    tokens = recv.shape[0]
    heads = recv.shape[1] // (4 * HD)
    own = lambda part: pl.BlockSpec((tokens, HD), lambda h, f, part=part: (0, part * heads + h))
    pair = pl.BlockSpec((2, tokens, HD), lambda h, f: (0, 0, h))
    head = pl.BlockSpec((tokens, HD), lambda h, f: (0, h))
    flops = 6 * SETS * 2 * tokens * TILE * HD * heads
    bytes_accessed = (4 * 2 + 4 * 4 + 4 * 2 * 2 + 2 * 2 + 2 * 4 + 4 * 2 * 2) * tokens * HD * heads
    out_shape = (
        jax.ShapeDtypeStruct((tokens, heads * HD), jnp.bfloat16),
        jax.ShapeDtypeStruct((tokens, heads * HD), jnp.bfloat16),
        jax.ShapeDtypeStruct((tokens, heads * HD), jnp.float32),
        jax.ShapeDtypeStruct((tokens, heads * HD), jnp.float32),
    ) + tuple(jax.ShapeDtypeStruct((2, tokens, heads * HD), jnp.bfloat16) for _ in range(4))
    return pl.pallas_call(
        _attn_kernel,
        out_shape=out_shape,
        grid_spec=pltpu.PrefetchScalarGridSpec(
            num_scalar_prefetch=1,
            grid=(heads,),
            in_specs=[own(0), own(3), own(1), own(2), pair, pair, pair, pair],
            out_specs=[head, head, head, head, pair, pair, pair, pair],
            scratch_shapes=[
                pltpu.VMEM((SETS, tokens, TILE), jnp.float32),
                pltpu.VMEM((SETS, tokens, TILE), jnp.float32),
            ],
        ),
        compiler_params=pltpu.CompilerParams(dimension_semantics=("arbitrary",)),
        cost_estimate=pl.CostEstimate(
            flops=flops, transcendentals=SETS * tokens * TILE * heads, bytes_accessed=bytes_accessed
        ),
    )(flags, recv, recv, recv, recv, kv_below, kv_above, kv_left, kv_right)


def shifted(block, axis, distance):
    devices = range(lax.axis_size(axis))
    route = [(i - distance, i) for i in devices if i - distance in devices]
    return lax.ppermute(block, axis, route)


def shards(query_rows, key_rows, value_rows, out_cotangent, tile_slot, window_reach):
    tokens_here, channels = query_rows.shape
    tm_count = lax.axis_size("tm")
    space_count = lax.axis_size("space")
    per_peer = tokens_here // (tm_count * space_count)
    own_rank = lax.axis_index("tm") * space_count + lax.axis_index("space")
    landing = tile_slot // tokens_here * per_peer + tile_slot % tokens_here - own_rank * per_peer
    chosen = (
        jnp.zeros((tokens_here,), jnp.int32)
        .at[landing]
        .set(jnp.arange(tokens_here, dtype=jnp.int32))
    )
    gathered = [rows[chosen] for rows in (query_rows, key_rows, value_rows, out_cotangent)]
    slab_index = lax.axis_index("tm")
    column = lax.axis_index("space")
    own_reach = lax.dynamic_index_in_dim(window_reach, slab_index, 0, keepdims=False)[0]
    flags = jnp.stack(
        [own_reach[0] > 0, own_reach[0] >= 0, own_reach[1] > 0, column > 0, column < space_count - 1]
    ).astype(jnp.int32)
    width = channels // CHUNKS
    backs = []
    gate = None
    for chunk in range(CHUNKS):
        cols = slice(chunk * width, (chunk + 1) * width)
        send = jnp.concatenate([rows[:, cols] for rows in gathered], axis=1)
        recv = lax.all_to_all(send, ("tm", "space"), split_axis=0, concat_axis=0, tiled=True)
        kv_own = jnp.stack([recv[:, width:2 * width], recv[:, 2 * width:3 * width]])
        if gate is not None:
            kv_own = lax.optimization_barrier((kv_own,) + gate)[0]
        halo = (
            shifted(kv_own, "tm", 1),
            shifted(kv_own, "tm", -1),
            shifted(kv_own, "space", 1),
            shifted(kv_own, "space", -1),
        )
        attended, query_grad, key_own, value_own, nb_b, nb_a, nb_l, nb_r = attend_tile(
            flags, recv, *halo
        )
        gate = halo
        early = jnp.concatenate([attended, query_grad], axis=1)
        if chunk + 1 < CHUNKS:
            early = lax.all_to_all(early, ("tm", "space"), split_axis=0, concat_axis=0, tiled=True)
        backs.append((early, key_own, value_own, nb_b, nb_a, nb_l, nb_r))
    outs = []
    prior = None
    for chunk in range(CHUNKS):
        early, key_own, value_own, nb_b, nb_a, nb_l, nb_r = backs[chunk]
        sends = (nb_b, nb_a, nb_l, nb_r)
        if prior is not None:
            sends = lax.optimization_barrier(sends + prior)[:4]
        elif CHUNKS > 1:
            sends = lax.optimization_barrier(sends + gate)[:4]
        nb_b, nb_a, nb_l, nb_r = sends
        received = (
            shifted(nb_b, "tm", -1),
            shifted(nb_a, "tm", 1),
            shifted(nb_l, "space", -1),
            shifted(nb_r, "space", 1),
        )
        prior = received
        terms = sum(part.astype(jnp.float32) for part in received)
        key_grad = (key_own + terms[0]).astype(jnp.bfloat16)
        value_grad = (value_own + terms[1]).astype(jnp.bfloat16)
        if chunk + 1 < CHUNKS:
            late = jnp.concatenate([key_grad, value_grad], axis=1)
            late = lax.all_to_all(late, ("tm", "space"), split_axis=0, concat_axis=0, tiled=True)
            outs.append(jnp.concatenate([early, late], axis=1))
        else:
            late = jnp.concatenate([early, key_grad, value_grad], axis=1)
            outs.append(lax.all_to_all(late, ("tm", "space"), split_axis=0, concat_axis=0, tiled=True))
    return tuple(
        jnp.concatenate([outs[chunk][:, i * width:(i + 1) * width] for chunk in range(CHUNKS)], axis=1)[landing]
        for i in range(4)
    )


def solution(mesh):
    return jax.shard_map(
        shards,
        mesh=mesh,
        in_specs=(
            P(("tm", "space"), None),
            P(("tm", "space"), None),
            P(("tm", "space"), None),
            P(("tm", "space"), None),
            P(("tm", "space")),
            P(None, "space", None),
        ),
        out_specs=(
            P(("tm", "space"), None),
            P(("tm", "space"), None),
            P(("tm", "space"), None),
            P(("tm", "space"), None),
        ),
        check_vma=False,
    )
```

```python
import functools

import jax
import jax.numpy as jnp
from jax import lax
from jax.experimental import pallas as pl
from jax.experimental.pallas import tpu as pltpu
from jax.sharding import PartitionSpec as P

H = 20
HD = 128
TILE = 256
SETS = 5
CHUNKS = 2
NT_DIMS = (((1,), (1,)), ((), ()))


def _attn_kernel(flags_ref, q_ref, g_ref, k_ref, v_ref, kb_ref, ka_ref, kl_ref, kr_ref,
                 o_ref, dq_ref, dko_ref, dvo_ref, nb_b, nb_a, nb_l, nb_r, s_scr, dp_scr):
    scale = HD ** (-0.5)
    q = q_ref[...]
    g = g_ref[...]
    keys = [kb_ref[0], k_ref[...], ka_ref[0], kl_ref[0], kr_ref[0]]
    vals = [kb_ref[1], v_ref[...], ka_ref[1], kl_ref[1], kr_ref[1]]
    nb_out = [nb_b, None, nb_a, nb_l, nb_r]
    vis = [flags_ref[a] > 0 for a in range(SETS)]

    m = jnp.full((TILE, 1), -1e30, jnp.float32)
    for a in range(SETS):
        s = lax.dot_general(q, keys[a], NT_DIMS, preferred_element_type=jnp.float32) * scale
        s = jnp.where(vis[a], s, -1e30)
        s_scr[a] = s
        m = jnp.maximum(m, jnp.max(s, axis=1, keepdims=True))
    l = jnp.zeros((TILE, 1), jnp.float32)
    for a in range(SETS):
        e = jnp.where(vis[a], jnp.exp(s_scr[a] - m), 0.0)
        s_scr[a] = e
        l = l + jnp.sum(e, axis=1, keepdims=True)
    inv = 1.0 / l
    o = jnp.zeros((TILE, HD), jnp.float32)
    rd = jnp.zeros((TILE, 1), jnp.float32)
    for a in range(SETS):
        p = s_scr[a] * inv
        pb = p.astype(jnp.bfloat16)
        o = o + jnp.dot(pb, vals[a], preferred_element_type=jnp.float32)
        dp = lax.dot_general(g, vals[a], NT_DIMS, preferred_element_type=jnp.float32)
        rd = rd + jnp.sum(p * dp, axis=1, keepdims=True)
        s_scr[a] = p
        dp_scr[a] = dp
        dv = jnp.dot(p.T.astype(jnp.bfloat16), g, preferred_element_type=jnp.float32)
        if a == 1:
            dvo_ref[...] = dv
        else:
            nb_out[a][1] = dv.astype(jnp.bfloat16)
    o_ref[...] = o.astype(jnp.bfloat16)
    dq = jnp.zeros((TILE, HD), jnp.float32)
    for a in range(SETS):
        ds = s_scr[a] * (dp_scr[a] - rd) * scale
        dq = dq + jnp.dot(ds.astype(jnp.bfloat16), keys[a], preferred_element_type=jnp.float32)
        dk = jnp.dot(ds.T.astype(jnp.bfloat16), q, preferred_element_type=jnp.float32)
        if a == 1:
            dko_ref[...] = dk
        else:
            nb_out[a][0] = dk.astype(jnp.bfloat16)
    dq_ref[...] = dq.astype(jnp.bfloat16)


def attend_tile(flags, recv, kv_below, kv_above, kv_left, kv_right):
    tokens = recv.shape[0]
    heads = recv.shape[1] // (4 * HD)
    own = lambda part: pl.BlockSpec((tokens, HD), lambda h, f, part=part: (0, part * heads + h))
    pair = pl.BlockSpec((2, tokens, HD), lambda h, f: (0, 0, h))
    head = pl.BlockSpec((tokens, HD), lambda h, f: (0, h))
    flops = 6 * SETS * 2 * tokens * TILE * HD * heads
    bytes_accessed = (4 * 2 + 4 * 4 + 4 * 2 * 2 + 2 * 2 + 2 * 4 + 4 * 2 * 2) * tokens * HD * heads
    out_shape = (
        jax.ShapeDtypeStruct((tokens, heads * HD), jnp.bfloat16),
        jax.ShapeDtypeStruct((tokens, heads * HD), jnp.bfloat16),
        jax.ShapeDtypeStruct((tokens, heads * HD), jnp.float32),
        jax.ShapeDtypeStruct((tokens, heads * HD), jnp.float32),
    ) + tuple(jax.ShapeDtypeStruct((2, tokens, heads * HD), jnp.bfloat16) for _ in range(4))
    return pl.pallas_call(
        _attn_kernel,
        out_shape=out_shape,
        grid_spec=pltpu.PrefetchScalarGridSpec(
            num_scalar_prefetch=1,
            grid=(heads,),
            in_specs=[own(0), own(3), own(1), own(2), pair, pair, pair, pair],
            out_specs=[head, head, head, head, pair, pair, pair, pair],
            scratch_shapes=[
                pltpu.VMEM((SETS, tokens, TILE), jnp.float32),
                pltpu.VMEM((SETS, tokens, TILE), jnp.float32),
            ],
        ),
        compiler_params=pltpu.CompilerParams(dimension_semantics=("arbitrary",)),
        cost_estimate=pl.CostEstimate(
            flops=flops, transcendentals=SETS * tokens * TILE * heads, bytes_accessed=bytes_accessed
        ),
    )(flags, recv, recv, recv, recv, kv_below, kv_above, kv_left, kv_right)


def shifted(block, axis, distance):
    devices = range(lax.axis_size(axis))
    route = [(i - distance, i) for i in devices if i - distance in devices]
    return lax.ppermute(block, axis, route)


def shards(query_rows, key_rows, value_rows, out_cotangent, tile_slot, window_reach):
    tokens_here, channels = query_rows.shape
    tm_count = lax.axis_size("tm")
    space_count = lax.axis_size("space")
    per_peer = tokens_here // (tm_count * space_count)
    own_rank = lax.axis_index("tm") * space_count + lax.axis_index("space")
    landing = tile_slot // tokens_here * per_peer + tile_slot % tokens_here - own_rank * per_peer
    chosen = (
        jnp.zeros((tokens_here,), jnp.int32)
        .at[landing]
        .set(jnp.arange(tokens_here, dtype=jnp.int32))
    )
    gathered = [rows[chosen] for rows in (query_rows, key_rows, value_rows, out_cotangent)]
    slab_index = lax.axis_index("tm")
    column = lax.axis_index("space")
    own_reach = lax.dynamic_index_in_dim(window_reach, slab_index, 0, keepdims=False)[0]
    flags = jnp.stack(
        [own_reach[0] > 0, own_reach[0] >= 0, own_reach[1] > 0, column > 0, column < space_count - 1]
    ).astype(jnp.int32)
    width = channels // CHUNKS
    backs = []
    gate = None
    for chunk in range(CHUNKS):
        cols = slice(chunk * width, (chunk + 1) * width)
        send = jnp.concatenate([rows[:, cols] for rows in gathered], axis=1)
        recv = lax.all_to_all(send, ("tm", "space"), split_axis=0, concat_axis=0, tiled=True)
        kv_own = jnp.stack([recv[:, width:2 * width], recv[:, 2 * width:3 * width]])
        if gate is not None:
            kv_own = lax.optimization_barrier((kv_own,) + gate)[0]
        halo = (
            shifted(kv_own, "tm", 1),
            shifted(kv_own, "tm", -1),
            shifted(kv_own, "space", 1),
            shifted(kv_own, "space", -1),
        )
        attended, query_grad, key_own, value_own, nb_b, nb_a, nb_l, nb_r = attend_tile(
            flags, recv, *halo
        )
        gate = halo
        early = jnp.concatenate([attended, query_grad], axis=1)
        early = lax.all_to_all(early, ("tm", "space"), split_axis=0, concat_axis=0, tiled=True)
        backs.append((early, key_own, value_own, nb_b, nb_a, nb_l, nb_r))
    outs = []
    prior = None
    for chunk in range(CHUNKS):
        early, key_own, value_own, nb_b, nb_a, nb_l, nb_r = backs[chunk]
        sends = (nb_b, nb_a, nb_l, nb_r)
        if prior is None and CHUNKS > 1:
            sends = lax.optimization_barrier(sends + gate)[:4]
        nb_b, nb_a, nb_l, nb_r = sends
        received = (
            shifted(nb_b, "tm", -1),
            shifted(nb_a, "tm", 1),
            shifted(nb_l, "space", -1),
            shifted(nb_r, "space", 1),
        )
        prior = received
        terms = sum(part.astype(jnp.float32) for part in received)
        key_grad = (key_own + terms[0]).astype(jnp.bfloat16)
        value_grad = (value_own + terms[1]).astype(jnp.bfloat16)
        late = jnp.concatenate([key_grad, value_grad], axis=1)
        late = lax.all_to_all(late, ("tm", "space"), split_axis=0, concat_axis=0, tiled=True)
        outs.append(jnp.concatenate([early, late], axis=1))
    return tuple(
        jnp.concatenate([outs[chunk][:, i * width:(i + 1) * width] for chunk in range(CHUNKS)], axis=1)[landing]
        for i in range(4)
    )


def solution(mesh):
    return jax.shard_map(
        shards,
        mesh=mesh,
        in_specs=(
            P(("tm", "space"), None),
            P(("tm", "space"), None),
            P(("tm", "space"), None),
            P(("tm", "space"), None),
            P(("tm", "space")),
            P(None, "space", None),
        ),
        out_specs=(
            P(("tm", "space"), None),
            P(("tm", "space"), None),
            P(("tm", "space"), None),
            P(("tm", "space"), None),
        ),
        check_vma=False,
    )
```

```python
import functools

import jax
import jax.numpy as jnp
from jax import lax
from jax.experimental import pallas as pl
from jax.experimental.pallas import tpu as pltpu
from jax.sharding import PartitionSpec as P

H = 20
HD = 128
TILE = 256
SETS = 5
CHUNKS = 2
NT_DIMS = (((1,), (1,)), ((), ()))
TN_DIMS = (((0,), (0,)), ((), ()))


def _attn_kernel(flags_ref, q_ref, g_ref, k_ref, v_ref, kb_ref, ka_ref, kl_ref, kr_ref,
                 o_ref, dq_ref, dko_ref, dvo_ref, nb_b, nb_a, nb_l, nb_r, s_scr, dp_scr):
    scale = HD ** (-0.5)
    q = q_ref[...]
    g = g_ref[...]
    keys = [kb_ref[0], k_ref[...], ka_ref[0], kl_ref[0], kr_ref[0]]
    vals = [kb_ref[1], v_ref[...], ka_ref[1], kl_ref[1], kr_ref[1]]
    nb_out = [nb_b, None, nb_a, nb_l, nb_r]
    vis = [flags_ref[a] > 0 for a in range(SETS)]

    m = jnp.full((TILE, 1), -1e30, jnp.float32)
    for a in range(SETS):
        s = lax.dot_general(q, keys[a], NT_DIMS, preferred_element_type=jnp.float32) * scale
        s = jnp.where(vis[a], s, -1e30)
        s_scr[a] = s
        m = jnp.maximum(m, jnp.max(s, axis=1, keepdims=True))
    l = jnp.zeros((TILE, 1), jnp.float32)
    for a in range(SETS):
        e = jnp.exp(s_scr[a] - m)
        s_scr[a] = e
        l = l + jnp.sum(e, axis=1, keepdims=True)
    inv = 1.0 / l
    o = jnp.zeros((TILE, HD), jnp.float32)
    rd = jnp.zeros((TILE, 1), jnp.float32)
    for a in range(SETS):
        p = s_scr[a] * inv
        pb = p.astype(jnp.bfloat16)
        o = o + jnp.dot(pb, vals[a], preferred_element_type=jnp.float32)
        dp = lax.dot_general(g, vals[a], NT_DIMS, preferred_element_type=jnp.float32)
        rd = rd + jnp.sum(p * dp, axis=1, keepdims=True)
        s_scr[a] = p
        dp_scr[a] = dp
        dv = lax.dot_general(pb, g, TN_DIMS, preferred_element_type=jnp.float32)
        if a == 1:
            dvo_ref[...] = dv
        else:
            nb_out[a][1] = dv.astype(jnp.bfloat16)
    o_ref[...] = o.astype(jnp.bfloat16)
    dq = jnp.zeros((TILE, HD), jnp.float32)
    for a in range(SETS):
        ds = (s_scr[a] * (dp_scr[a] - rd) * scale).astype(jnp.bfloat16)
        dq = dq + jnp.dot(ds, keys[a], preferred_element_type=jnp.float32)
        dk = lax.dot_general(ds, q, TN_DIMS, preferred_element_type=jnp.float32)
        if a == 1:
            dko_ref[...] = dk
        else:
            nb_out[a][0] = dk.astype(jnp.bfloat16)
    dq_ref[...] = dq.astype(jnp.bfloat16)


def attend_tile(flags, recv, kv_below, kv_above, kv_left, kv_right):
    tokens = recv.shape[0]
    heads = recv.shape[1] // (4 * HD)
    own = lambda part: pl.BlockSpec((tokens, HD), lambda h, f, part=part: (0, part * heads + h))
    pair = pl.BlockSpec((2, tokens, HD), lambda h, f: (0, 0, h))
    head = pl.BlockSpec((tokens, HD), lambda h, f: (0, h))
    flops = 6 * SETS * 2 * tokens * TILE * HD * heads
    bytes_accessed = (4 * 2 + 4 * 4 + 4 * 2 * 2 + 2 * 2 + 2 * 4 + 4 * 2 * 2) * tokens * HD * heads
    out_shape = (
        jax.ShapeDtypeStruct((tokens, heads * HD), jnp.bfloat16),
        jax.ShapeDtypeStruct((tokens, heads * HD), jnp.bfloat16),
        jax.ShapeDtypeStruct((tokens, heads * HD), jnp.float32),
        jax.ShapeDtypeStruct((tokens, heads * HD), jnp.float32),
    ) + tuple(jax.ShapeDtypeStruct((2, tokens, heads * HD), jnp.bfloat16) for _ in range(4))
    return pl.pallas_call(
        _attn_kernel,
        out_shape=out_shape,
        grid_spec=pltpu.PrefetchScalarGridSpec(
            num_scalar_prefetch=1,
            grid=(heads,),
            in_specs=[own(0), own(3), own(1), own(2), pair, pair, pair, pair],
            out_specs=[head, head, head, head, pair, pair, pair, pair],
            scratch_shapes=[
                pltpu.VMEM((SETS, tokens, TILE), jnp.float32),
                pltpu.VMEM((SETS, tokens, TILE), jnp.float32),
            ],
        ),
        compiler_params=pltpu.CompilerParams(dimension_semantics=("arbitrary",)),
        cost_estimate=pl.CostEstimate(
            flops=flops, transcendentals=SETS * tokens * TILE * heads, bytes_accessed=bytes_accessed
        ),
    )(flags, recv, recv, recv, recv, kv_below, kv_above, kv_left, kv_right)


def shifted(block, axis, distance):
    devices = range(lax.axis_size(axis))
    route = [(i - distance, i) for i in devices if i - distance in devices]
    return lax.ppermute(block, axis, route)


def shards(query_rows, key_rows, value_rows, out_cotangent, tile_slot, window_reach):
    tokens_here, channels = query_rows.shape
    tm_count = lax.axis_size("tm")
    space_count = lax.axis_size("space")
    per_peer = tokens_here // (tm_count * space_count)
    own_rank = lax.axis_index("tm") * space_count + lax.axis_index("space")
    landing = tile_slot // tokens_here * per_peer + tile_slot % tokens_here - own_rank * per_peer
    chosen = (
        jnp.zeros((tokens_here,), jnp.int32)
        .at[landing]
        .set(jnp.arange(tokens_here, dtype=jnp.int32))
    )
    gathered = [rows[chosen] for rows in (query_rows, key_rows, value_rows, out_cotangent)]
    slab_index = lax.axis_index("tm")
    column = lax.axis_index("space")
    own_reach = lax.dynamic_index_in_dim(window_reach, slab_index, 0, keepdims=False)[0]
    flags = jnp.stack(
        [own_reach[0] > 0, own_reach[0] >= 0, own_reach[1] > 0, column > 0, column < space_count - 1]
    ).astype(jnp.int32)
    width = channels // CHUNKS
    backs = []
    gate = None
    for chunk in range(CHUNKS):
        cols = slice(chunk * width, (chunk + 1) * width)
        send = jnp.concatenate([rows[:, cols] for rows in gathered], axis=1)
        recv = lax.all_to_all(send, ("tm", "space"), split_axis=0, concat_axis=0, tiled=True)
        kv_own = jnp.stack([recv[:, width:2 * width], recv[:, 2 * width:3 * width]])
        if gate is not None:
            kv_own = lax.optimization_barrier((kv_own,) + gate)[0]
        halo = (
            shifted(kv_own, "tm", 1),
            shifted(kv_own, "tm", -1),
            shifted(kv_own, "space", 1),
            shifted(kv_own, "space", -1),
        )
        attended, query_grad, key_own, value_own, nb_b, nb_a, nb_l, nb_r = attend_tile(
            flags, recv, *halo
        )
        gate = halo
        early = jnp.concatenate([attended, query_grad], axis=1)
        early = lax.all_to_all(early, ("tm", "space"), split_axis=0, concat_axis=0, tiled=True)
        backs.append((early, key_own, value_own, nb_b, nb_a, nb_l, nb_r))
    outs = []
    prior = None
    for chunk in range(CHUNKS):
        early, key_own, value_own, nb_b, nb_a, nb_l, nb_r = backs[chunk]
        sends = (nb_b, nb_a, nb_l, nb_r)
        if prior is None and CHUNKS > 1:
            sends = lax.optimization_barrier(sends + gate)[:4]
        nb_b, nb_a, nb_l, nb_r = sends
        received = (
            shifted(nb_b, "tm", -1),
            shifted(nb_a, "tm", 1),
            shifted(nb_l, "space", -1),
            shifted(nb_r, "space", 1),
        )
        prior = received
        terms = sum(part.astype(jnp.float32) for part in received)
        key_grad = (key_own + terms[0]).astype(jnp.bfloat16)
        value_grad = (value_own + terms[1]).astype(jnp.bfloat16)
        late = jnp.concatenate([key_grad, value_grad], axis=1)
        late = lax.all_to_all(late, ("tm", "space"), split_axis=0, concat_axis=0, tiled=True)
        outs.append(jnp.concatenate([early, late], axis=1))
    return tuple(
        jnp.concatenate([outs[chunk][:, i * width:(i + 1) * width] for chunk in range(CHUNKS)], axis=1)[landing]
        for i in range(4)
    )


def solution(mesh):
    return jax.shard_map(
        shards,
        mesh=mesh,
        in_specs=(
            P(("tm", "space"), None),
            P(("tm", "space"), None),
            P(("tm", "space"), None),
            P(("tm", "space"), None),
            P(("tm", "space")),
            P(None, "space", None),
        ),
        out_specs=(
            P(("tm", "space"), None),
            P(("tm", "space"), None),
            P(("tm", "space"), None),
            P(("tm", "space"), None),
        ),
        check_vma=False,
    )
```

```python
import functools

import jax
import jax.numpy as jnp
from jax import lax
from jax.experimental import pallas as pl
from jax.experimental.pallas import tpu as pltpu
from jax.sharding import PartitionSpec as P

H = 20
HD = 128
TILE = 256
SETS = 5
CHUNKS = 2
HEAD_SPLIT = (8, 12)
NT_DIMS = (((1,), (1,)), ((), ()))
TN_DIMS = (((0,), (0,)), ((), ()))


def _attn_kernel(flags_ref, q_ref, g_ref, k_ref, v_ref, kb_ref, ka_ref, kl_ref, kr_ref,
                 o_ref, dq_ref, dko_ref, dvo_ref, nb_b, nb_a, nb_l, nb_r, s_scr, dp_scr):
    scale = HD ** (-0.5)
    q = q_ref[...]
    g = g_ref[...]
    keys = [kb_ref[0], k_ref[...], ka_ref[0], kl_ref[0], kr_ref[0]]
    vals = [kb_ref[1], v_ref[...], ka_ref[1], kl_ref[1], kr_ref[1]]
    nb_out = [nb_b, None, nb_a, nb_l, nb_r]
    vis = [flags_ref[a] > 0 for a in range(SETS)]

    m = jnp.full((TILE, 1), -1e30, jnp.float32)
    for a in range(SETS):
        s = lax.dot_general(q, keys[a], NT_DIMS, preferred_element_type=jnp.float32) * scale
        s = jnp.where(vis[a], s, -1e30)
        s_scr[a] = s
        m = jnp.maximum(m, jnp.max(s, axis=1, keepdims=True))
    l = jnp.zeros((TILE, 1), jnp.float32)
    for a in range(SETS):
        e = jnp.exp(s_scr[a] - m)
        s_scr[a] = e
        l = l + jnp.sum(e, axis=1, keepdims=True)
    inv = 1.0 / l
    o = jnp.zeros((TILE, HD), jnp.float32)
    rd = jnp.zeros((TILE, 1), jnp.float32)
    for a in range(SETS):
        p = s_scr[a] * inv
        pb = p.astype(jnp.bfloat16)
        o = o + jnp.dot(pb, vals[a], preferred_element_type=jnp.float32)
        dp = lax.dot_general(g, vals[a], NT_DIMS, preferred_element_type=jnp.float32)
        rd = rd + jnp.sum(p * dp, axis=1, keepdims=True)
        s_scr[a] = p
        dp_scr[a] = dp
        dv = lax.dot_general(pb, g, TN_DIMS, preferred_element_type=jnp.float32)
        if a == 1:
            dvo_ref[...] = dv
        else:
            nb_out[a][1] = dv.astype(jnp.bfloat16)
    o_ref[...] = o.astype(jnp.bfloat16)
    dq = jnp.zeros((TILE, HD), jnp.float32)
    for a in range(SETS):
        ds = (s_scr[a] * (dp_scr[a] - rd) * scale).astype(jnp.bfloat16)
        dq = dq + jnp.dot(ds, keys[a], preferred_element_type=jnp.float32)
        dk = lax.dot_general(ds, q, TN_DIMS, preferred_element_type=jnp.float32)
        if a == 1:
            dko_ref[...] = dk
        else:
            nb_out[a][0] = dk.astype(jnp.bfloat16)
    dq_ref[...] = dq.astype(jnp.bfloat16)


def attend_tile(flags, recv, kv_below, kv_above, kv_left, kv_right):
    tokens = recv.shape[0]
    heads = recv.shape[1] // (4 * HD)
    own = lambda part: pl.BlockSpec((tokens, HD), lambda h, f, part=part: (0, part * heads + h))
    pair = pl.BlockSpec((2, tokens, HD), lambda h, f: (0, 0, h))
    head = pl.BlockSpec((tokens, HD), lambda h, f: (0, h))
    flops = 6 * SETS * 2 * tokens * TILE * HD * heads
    bytes_accessed = (4 * 2 + 4 * 4 + 4 * 2 * 2 + 2 * 2 + 2 * 4 + 4 * 2 * 2) * tokens * HD * heads
    out_shape = (
        jax.ShapeDtypeStruct((tokens, heads * HD), jnp.bfloat16),
        jax.ShapeDtypeStruct((tokens, heads * HD), jnp.bfloat16),
        jax.ShapeDtypeStruct((tokens, heads * HD), jnp.float32),
        jax.ShapeDtypeStruct((tokens, heads * HD), jnp.float32),
    ) + tuple(jax.ShapeDtypeStruct((2, tokens, heads * HD), jnp.bfloat16) for _ in range(4))
    return pl.pallas_call(
        _attn_kernel,
        out_shape=out_shape,
        grid_spec=pltpu.PrefetchScalarGridSpec(
            num_scalar_prefetch=1,
            grid=(heads,),
            in_specs=[own(0), own(3), own(1), own(2), pair, pair, pair, pair],
            out_specs=[head, head, head, head, pair, pair, pair, pair],
            scratch_shapes=[
                pltpu.VMEM((SETS, tokens, TILE), jnp.float32),
                pltpu.VMEM((SETS, tokens, TILE), jnp.float32),
            ],
        ),
        compiler_params=pltpu.CompilerParams(dimension_semantics=("arbitrary",)),
        cost_estimate=pl.CostEstimate(
            flops=flops, transcendentals=SETS * tokens * TILE * heads, bytes_accessed=bytes_accessed
        ),
    )(flags, recv, recv, recv, recv, kv_below, kv_above, kv_left, kv_right)


def shifted(block, axis, distance):
    devices = range(lax.axis_size(axis))
    route = [(i - distance, i) for i in devices if i - distance in devices]
    return lax.ppermute(block, axis, route)


def shards(query_rows, key_rows, value_rows, out_cotangent, tile_slot, window_reach):
    tokens_here, channels = query_rows.shape
    tm_count = lax.axis_size("tm")
    space_count = lax.axis_size("space")
    per_peer = tokens_here // (tm_count * space_count)
    own_rank = lax.axis_index("tm") * space_count + lax.axis_index("space")
    landing = tile_slot // tokens_here * per_peer + tile_slot % tokens_here - own_rank * per_peer
    chosen = (
        jnp.zeros((tokens_here,), jnp.int32)
        .at[landing]
        .set(jnp.arange(tokens_here, dtype=jnp.int32))
    )
    gathered = [rows[chosen] for rows in (query_rows, key_rows, value_rows, out_cotangent)]
    slab_index = lax.axis_index("tm")
    column = lax.axis_index("space")
    own_reach = lax.dynamic_index_in_dim(window_reach, slab_index, 0, keepdims=False)[0]
    flags = jnp.stack(
        [own_reach[0] > 0, own_reach[0] >= 0, own_reach[1] > 0, column > 0, column < space_count - 1]
    ).astype(jnp.int32)
    starts = [sum(HEAD_SPLIT[:c]) * HD for c in range(CHUNKS)]
    widths = [n * HD for n in HEAD_SPLIT]
    backs = []
    gate = None
    for chunk in range(CHUNKS):
        width = widths[chunk]
        cols = slice(starts[chunk], starts[chunk] + width)
        send = jnp.concatenate([rows[:, cols] for rows in gathered], axis=1)
        recv = lax.all_to_all(send, ("tm", "space"), split_axis=0, concat_axis=0, tiled=True)
        kv_own = jnp.stack([recv[:, width:2 * width], recv[:, 2 * width:3 * width]])
        if gate is not None:
            kv_own = lax.optimization_barrier((kv_own,) + gate)[0]
        halo = (
            shifted(kv_own, "tm", 1),
            shifted(kv_own, "tm", -1),
            shifted(kv_own, "space", 1),
            shifted(kv_own, "space", -1),
        )
        attended, query_grad, key_own, value_own, nb_b, nb_a, nb_l, nb_r = attend_tile(
            flags, recv, *halo
        )
        gate = halo
        early = jnp.concatenate([attended, query_grad], axis=1)
        early = lax.all_to_all(early, ("tm", "space"), split_axis=0, concat_axis=0, tiled=True)
        backs.append((early, key_own, value_own, nb_b, nb_a, nb_l, nb_r))
    outs = []
    prior = None
    for chunk in range(CHUNKS):
        early, key_own, value_own, nb_b, nb_a, nb_l, nb_r = backs[chunk]
        width = widths[chunk]
        sends = (nb_b, nb_a, nb_l, nb_r)
        if prior is None and CHUNKS > 1:
            sends = lax.optimization_barrier(sends + gate)[:4]
        nb_b, nb_a, nb_l, nb_r = sends
        received = (
            shifted(nb_b, "tm", -1),
            shifted(nb_a, "tm", 1),
            shifted(nb_l, "space", -1),
            shifted(nb_r, "space", 1),
        )
        prior = received
        terms = sum(part.astype(jnp.float32) for part in received)
        key_grad = (key_own + terms[0]).astype(jnp.bfloat16)
        value_grad = (value_own + terms[1]).astype(jnp.bfloat16)
        late = jnp.concatenate([key_grad, value_grad], axis=1)
        late = lax.all_to_all(late, ("tm", "space"), split_axis=0, concat_axis=0, tiled=True)
        outs.append(jnp.concatenate([early, late], axis=1))
    return tuple(
        jnp.concatenate(
            [outs[chunk][:, i * widths[chunk]:(i + 1) * widths[chunk]] for chunk in range(CHUNKS)], axis=1
        )[landing]
        for i in range(4)
    )


def solution(mesh):
    return jax.shard_map(
        shards,
        mesh=mesh,
        in_specs=(
            P(("tm", "space"), None),
            P(("tm", "space"), None),
            P(("tm", "space"), None),
            P(("tm", "space"), None),
            P(("tm", "space")),
            P(None, "space", None),
        ),
        out_specs=(
            P(("tm", "space"), None),
            P(("tm", "space"), None),
            P(("tm", "space"), None),
            P(("tm", "space"), None),
        ),
        check_vma=False,
    )
```
